256 devices in a mesh: shard: 64 (over y, z_hi, x), rep: 4 (over z_lo, core).
Axes of the slice: x: 4, y: 4, z: 8 (z_hi: 4, z_lo: 2; z = z_hi * 2 + z_lo), core: 2. Of those that a mesh axis runs over, the one named last changes fastest.
Arguments:
- rows_in: bfloat16 [131072, 2048], P(('shard', 'rep')), may hold values from -24 to 24
- cotangent: bfloat16 [131072, 2048], P(('shard', 'rep')), may hold values from -24 to 24
- expert_counts: int32 [256, 2], P(('shard', 'rep')), may hold values from 0 to 512, as said below
- weights: bfloat16 [2048, 2, 1152], P('shard'), may hold values from -0.125 to 0.125
Outputs:
- rows_out: bfloat16 [131072, 2048], P(('shard', 'rep'))
- rows_grad: bfloat16 [131072, 2048], P(('shard', 'rep'))
- weight_grad: float32 [2048, 2, 1152], P('shard')
The draws below stay inside these ranges and needn't reach their ends.
Inputs may be any that keep to these rules, and one draw needn't show every extreme that they name: `expert_counts`: on each device the experts' regions, each padded to a multiple of 128 rows, follow one another from row 0 and together fill at most 512 rows; some device fills all 512; one expert on some device holds all 512 rows.
All inputs are finite; a program needn't handle non-finite values.
Results may differ from the reference program's by a relative error of at most 0.0095.
Values may be sent and summed in bfloat16 or wider, within the bound.
No kernel may reach another device: no remote copies, remote signals or barrier semaphores. Data moves between devices by JAX's collectives and lax.ppermute only.
A program may use at most 128 MiB of HBM per device.

```python
import jax
import jax.numpy as jnp
from jax import lax

D = 2048
FF = 384
G = 2
BLOCK = 128
ROWS_DEV = 512
NDEV = 256
ROWS = 131072


def draw_expert_counts(key, part):
    nblocks = ROWS_DEV // BLOCK
    key_total, key_full, key_first, key_tail = jax.random.split(key, 4)
    totals = jax.random.randint(key_total, (NDEV,), 1, nblocks + 1)
    fuller = jax.random.randint(key_full, (), 0, NDEV)
    is_fuller = jnp.arange(NDEV) == fuller
    totals = jnp.where(is_fuller, nblocks, totals)
    firsts = jax.random.randint(key_first, (NDEV,), 0, totals + 1)
    firsts = jnp.where(is_fuller, nblocks, firsts)
    blocks = jnp.stack([firsts, totals - firsts], axis=1)
    tails = jax.random.randint(key_tail, (NDEV, G), 1, BLOCK + 1)
    tails = jnp.where(is_fuller[:, None], BLOCK, tails)
    counts = jnp.where(blocks > 0, (blocks - 1) * BLOCK + tails, 0)
    return counts.astype(jnp.int32)


def raised(result, key, source, target, shards_of, factor):
    owner, partner = [(jnp.arange(result.shape[axis_at]) // (result.shape[axis_at] // shards_of)).reshape([-1 if axis == axis_at else 1 for axis in range(result.ndim)]) for axis_at in (source, target)]
    chosen = jax.random.permutation(key, shards_of)[partner]
    strong = (owner == chosen) | (owner == (partner + shards_of // 2) % shards_of)
    return jnp.where(strong, factor * result, result)


def block_levels(rng, shape, pieces, low, top_value):
    factor_of, own = 1.0, jax.random.fold_in(rng, 6)
    for dim, parts in pieces:
        draws = jnp.exp(jax.random.uniform(jax.random.fold_in(own, dim), (parts,), jnp.float32, low / len(pieces), top_value / len(pieces)))
        factor_of = factor_of * jnp.repeat(draws, shape[dim] // parts).reshape([-1 if axis == dim else 1 for axis in range(len(shape))])
    return factor_of


def scatter_about(key, shape, width, reach, shards=(), kind=jnp.bfloat16):
    values = jax.random.normal(key, shape, jnp.float32) * width
    if len(shards) > 0:
        values = block_levels(key, shape, shards, -0.22, 0.18) * values
    return jnp.clip(values, min=-reach, max=reach).astype(kind)


def heavy_noise(stream_key, extent, scale, most, pieces, heavy, kind=jnp.bfloat16):
    entries = scale * jax.random.normal(stream_key, extent, jnp.float32)
    if pieces:
        entries = entries * block_levels(stream_key, extent, pieces, -0.22, 0.18)
    return jnp.clip(raised(entries, jax.random.fold_in(stream_key, 3), *heavy), -most, most).astype(kind)


def setup_inputs(seed: int = 0) -> dict:
    splits = jax.random.split(jax.random.key(seed), 5)
    return {
        "rows_in": heavy_noise(splits[0], (ROWS, D), 1.0, 24.0, ((0, 256),), (0, 1, 256, 6.0)),
        "cotangent": heavy_noise(splits[1], (ROWS, D), 1.0, 24.0, ((0, 256),), (0, 1, 256, 6.0)),
        "expert_counts": draw_expert_counts(jax.random.fold_in(splits[4], 71), 0),
        "weights": scatter_about(splits[3], (D, G, 3 * FF), D ** -0.5, 0.125, ((0, 64),)),
    }


def expert_block(inputs, upstream, expert_slab):
    hidden_width = expert_slab.shape[1] // 3
    gate_up = expert_slab[:, :2 * hidden_width]
    down_t = expert_slab[:, 2 * hidden_width:]
    project = jnp.dot(inputs, gate_up, preferred_element_type=jnp.float32)
    gate_pre = project[:, :hidden_width]
    up_pre = project[:, hidden_width:]
    gate_sigmoid = jax.nn.sigmoid(gate_pre)
    active = gate_pre * gate_sigmoid
    hidden = (active * up_pre).astype(jnp.bfloat16)
    output = lax.dot_general(hidden, down_t, (((1,), (1,)), ((), ())), preferred_element_type=jnp.float32).astype(jnp.bfloat16)
    hidden_grad = jnp.dot(upstream, down_t, preferred_element_type=jnp.float32)
    down_grad = lax.dot_general(upstream, hidden, (((0,), (0,)), ((), ())), preferred_element_type=jnp.float32)
    gate_grad = hidden_grad * up_pre * gate_sigmoid * (1.0 + gate_pre * (1.0 - gate_sigmoid))
    up_grad = hidden_grad * active
    joint_grad = jnp.concatenate([gate_grad, up_grad], axis=1).astype(jnp.bfloat16)
    proj_grad = lax.dot_general(inputs, joint_grad, (((0,), (0,)), ((), ())), preferred_element_type=jnp.float32)
    input_grad = lax.dot_general(joint_grad, gate_up, (((1,), (1,)), ((), ())), preferred_element_type=jnp.float32).astype(jnp.bfloat16)
    return output, input_grad, jnp.concatenate([proj_grad, down_grad], axis=1)


def alive_rows(counts, total_rows):
    padded = (counts + BLOCK - 1) // BLOCK * BLOCK
    starts = jnp.cumsum(padded) - padded
    position = jnp.arange(total_rows, dtype=jnp.int32)
    inside = (position[:, None] >= starts[None, :]) & (position[:, None] < (starts + counts)[None, :])
    return jnp.any(inside, axis=1), padded, starts


def reference(rows_in, cotangent, expert_counts, weights):
    def device_pass(grad_carry, device_items):
        inputs, upstream, counts = device_items
        alive, padded, starts = alive_rows(counts, ROWS_DEV)
        inputs = jnp.where(alive[:, None], inputs, jnp.zeros_like(inputs))
        upstream = jnp.where(alive[:, None], upstream, jnp.zeros_like(upstream))

        def block_pass(grad_total, block_index):
            row_begin = (block_index * BLOCK).astype(jnp.int32)
            owner_index = (jnp.sum((starts <= row_begin).astype(jnp.int32)) - 1).astype(jnp.int32)
            expert_slab = lax.dynamic_index_in_dim(weights, owner_index, 1, keepdims=False)
            block_in = lax.dynamic_slice_in_dim(inputs, row_begin, BLOCK, 0)
            block_up = lax.dynamic_slice_in_dim(upstream, row_begin, BLOCK, 0)
            output, input_grad, grad_piece = expert_block(block_in, block_up, expert_slab)
            current = lax.dynamic_index_in_dim(grad_total, owner_index, 1, keepdims=False)
            grad_total = lax.dynamic_update_index_in_dim(grad_total, current + grad_piece, owner_index, 1)
            return grad_total, (output, input_grad)

        grad_carry, (outputs, input_grads) = lax.scan(block_pass, grad_carry, jnp.arange(ROWS_DEV // BLOCK, dtype=jnp.int32))
        return grad_carry, (outputs.reshape(ROWS_DEV, D), input_grads.reshape(ROWS_DEV, D))

    start_grad = jnp.zeros((D, G, 3 * FF), jnp.float32)
    device_rows = rows_in.reshape(NDEV, ROWS_DEV, D)
    device_cots = cotangent.reshape(NDEV, ROWS_DEV, D)
    weight_grad, (rows_out, rows_grad) = lax.scan(device_pass, start_grad, (device_rows, device_cots, expert_counts))
    return rows_out.reshape(ROWS, D), rows_grad.reshape(ROWS, D), weight_grad
```

```python
import jax
import jax.numpy as jnp
from jax import lax
from jax.sharding import PartitionSpec as P

BLOCK = 128


def expert_block(inputs, upstream, expert_slab):
    hidden_width = expert_slab.shape[1] // 3
    gate_up = expert_slab[:, : 2 * hidden_width]
    down_t = expert_slab[:, 2 * hidden_width :]
    project = jnp.dot(inputs, gate_up, preferred_element_type=jnp.float32)
    gate_pre = project[:, :hidden_width]
    up_pre = project[:, hidden_width:]
    gate_sigmoid = jax.nn.sigmoid(gate_pre)
    active = gate_pre * gate_sigmoid
    hidden = (active * up_pre).astype(jnp.bfloat16)
    output = lax.dot_general(
        hidden, down_t, (((1,), (1,)), ((), ())), preferred_element_type=jnp.float32
    ).astype(jnp.bfloat16)
    hidden_grad = jnp.dot(upstream, down_t, preferred_element_type=jnp.float32)
    down_grad = lax.dot_general(
        upstream, hidden, (((0,), (0,)), ((), ())), preferred_element_type=jnp.float32
    )
    gate_grad = hidden_grad * up_pre * gate_sigmoid * (1.0 + gate_pre * (1.0 - gate_sigmoid))
    up_grad = hidden_grad * active
    joint_grad = jnp.concatenate([gate_grad, up_grad], axis=1).astype(jnp.bfloat16)
    proj_grad = lax.dot_general(
        inputs, joint_grad, (((0,), (0,)), ((), ())), preferred_element_type=jnp.float32
    )
    input_grad = lax.dot_general(
        joint_grad, gate_up, (((1,), (1,)), ((), ())), preferred_element_type=jnp.float32
    ).astype(jnp.bfloat16)
    return (output, input_grad, jnp.concatenate([proj_grad, down_grad], axis=1))


def alive_rows(counts, total_rows):
    padded = (counts + BLOCK - 1) // BLOCK * BLOCK
    starts = jnp.cumsum(padded) - padded
    position = jnp.arange(total_rows, dtype=jnp.int32)
    inside = (position[:, None] >= starts[None, :]) & (
        position[:, None] < (starts + counts)[None, :]
    )
    return (jnp.any(inside, axis=1), padded, starts)


def run_expert(expert_slab, inputs, upstream, start_row, nblocks, outputs, input_grads):

    def block_step(block_index, state):
        outputs, input_grads, grad_total = state
        row_begin = start_row + block_index * BLOCK
        block_in = lax.dynamic_slice_in_dim(inputs, row_begin, BLOCK, 0)
        block_up = lax.dynamic_slice_in_dim(upstream, row_begin, BLOCK, 0)
        output, input_grad, grad_piece = expert_block(block_in, block_up, expert_slab)
        outputs = lax.dynamic_update_slice_in_dim(outputs, output, row_begin, 0)
        input_grads = lax.dynamic_update_slice_in_dim(input_grads, input_grad, row_begin, 0)
        return (outputs, input_grads, grad_total + grad_piece)

    start_grad = jnp.zeros(expert_slab.shape, jnp.float32)
    return lax.fori_loop(jnp.int32(0), nblocks, block_step, (outputs, input_grads, start_grad))


def core_pairs(n):
    return [(i, i ^ 1) for i in range(n)]


def chip_pairs(n):
    return [(i, i ^ 2) for i in range(n)]


def local(rows_in, cotangent, expert_counts, weights):
    nrep = lax.axis_size("rep")
    core = lax.axis_index("rep") % 2
    other = 1 - core
    counts = expert_counts[0]
    alive, padded, starts = alive_rows(counts, rows_in.shape[0])
    inputs = jnp.where(alive[:, None], rows_in, jnp.zeros_like(rows_in))
    upstream = jnp.where(alive[:, None], cotangent, jnp.zeros_like(cotangent))
    outputs = jnp.zeros_like(rows_in)
    input_grads = jnp.zeros_like(rows_in)

    mine_local = lax.dynamic_index_in_dim(weights, core, 1, keepdims=False)
    mine = lax.all_gather(mine_local, "shard", axis=0, tiled=True)
    theirs = lax.ppermute(mine, "rep", core_pairs(nrep))

    outputs, input_grads, grad_mine = run_expert(
        mine, inputs, upstream, starts[core], padded[core] // BLOCK, outputs, input_grads
    )
    outputs, input_grads, grad_theirs = run_expert(
        theirs, inputs, upstream, starts[other], padded[other] // BLOCK, outputs, input_grads
    )
    grad_mine = grad_mine + lax.ppermute(grad_theirs, "rep", core_pairs(nrep))
    part = lax.psum_scatter(grad_mine, "shard", scatter_dimension=0, tiled=True)
    part = part + lax.ppermute(part, "rep", chip_pairs(nrep))
    part_other = lax.ppermute(part, "rep", core_pairs(nrep))
    first = jnp.where(core == 0, part, part_other)
    second = jnp.where(core == 0, part_other, part)
    reduced = jnp.stack([first, second], axis=1)
    return (outputs, input_grads, reduced)


def solution(mesh):
    in_specs = (
        P(("shard", "rep"), None),
        P(("shard", "rep"), None),
        P(("shard", "rep"), None),
        P("shard", None, None),
    )
    out_specs = (P(("shard", "rep"), None), P(("shard", "rep"), None), P("shard", None, None))
    return jax.shard_map(local, mesh=mesh, in_specs=in_specs, out_specs=out_specs, check_vma=False)
```

```python
import jax
import jax.numpy as jnp
import numpy as np
from jax import lax
from jax.sharding import Mesh
from jax.sharding import PartitionSpec as P

BLOCK = 128


def expert_block(inputs, upstream, expert_slab):
    hidden_width = expert_slab.shape[1] // 3
    gate_up = expert_slab[:, : 2 * hidden_width]
    down_t = expert_slab[:, 2 * hidden_width :]
    project = jnp.dot(inputs, gate_up, preferred_element_type=jnp.float32)
    gate_pre = project[:, :hidden_width]
    up_pre = project[:, hidden_width:]
    gate_sigmoid = jax.nn.sigmoid(gate_pre)
    active = gate_pre * gate_sigmoid
    hidden = (active * up_pre).astype(jnp.bfloat16)
    output = lax.dot_general(
        hidden, down_t, (((1,), (1,)), ((), ())), preferred_element_type=jnp.float32
    ).astype(jnp.bfloat16)
    hidden_grad = jnp.dot(upstream, down_t, preferred_element_type=jnp.float32)
    down_grad = lax.dot_general(
        upstream, hidden, (((0,), (0,)), ((), ())), preferred_element_type=jnp.float32
    )
    gate_grad = hidden_grad * up_pre * gate_sigmoid * (1.0 + gate_pre * (1.0 - gate_sigmoid))
    up_grad = hidden_grad * active
    joint_grad = jnp.concatenate([gate_grad, up_grad], axis=1).astype(jnp.bfloat16)
    proj_grad = lax.dot_general(
        inputs, joint_grad, (((0,), (0,)), ((), ())), preferred_element_type=jnp.float32
    )
    input_grad = lax.dot_general(
        joint_grad, gate_up, (((1,), (1,)), ((), ())), preferred_element_type=jnp.float32
    ).astype(jnp.bfloat16)
    return (output, input_grad, jnp.concatenate([proj_grad, down_grad], axis=1))


def alive_rows(counts, total_rows):
    padded = (counts + BLOCK - 1) // BLOCK * BLOCK
    starts = jnp.cumsum(padded) - padded
    position = jnp.arange(total_rows, dtype=jnp.int32)
    inside = (position[:, None] >= starts[None, :]) & (
        position[:, None] < (starts + counts)[None, :]
    )
    return (jnp.any(inside, axis=1), padded, starts)


def run_expert(expert_slab, inputs, upstream, start_row, nblocks, outputs, input_grads):

    def block_step(block_index, state):
        outputs, input_grads, grad_total = state
        row_begin = start_row + block_index * BLOCK
        block_in = lax.dynamic_slice_in_dim(inputs, row_begin, BLOCK, 0)
        block_up = lax.dynamic_slice_in_dim(upstream, row_begin, BLOCK, 0)
        output, input_grad, grad_piece = expert_block(block_in, block_up, expert_slab)
        outputs = lax.dynamic_update_slice_in_dim(outputs, output, row_begin, 0)
        input_grads = lax.dynamic_update_slice_in_dim(input_grads, input_grad, row_begin, 0)
        return (outputs, input_grads, grad_total + grad_piece)

    start_grad = jnp.zeros(expert_slab.shape, jnp.float32)
    return lax.fori_loop(jnp.int32(0), nblocks, block_step, (outputs, input_grads, start_grad))


SHARD = ("y", "zh", "x")
REP = ("zl", "c")


def core_pairs(n):
    return [(i, i ^ 1) for i in range(n)]


def chip_pairs(n):
    return [(i, i ^ 2) for i in range(n)]


def local(rows_in, cotangent, expert_counts, weights):
    nrep = lax.axis_size(REP)
    core = lax.axis_index("c")
    other = 1 - core
    counts = expert_counts[0]
    alive, padded, starts = alive_rows(counts, rows_in.shape[0])
    inputs = jnp.where(alive[:, None], rows_in, jnp.zeros_like(rows_in))
    upstream = jnp.where(alive[:, None], cotangent, jnp.zeros_like(cotangent))
    outputs = jnp.zeros_like(rows_in)
    input_grads = jnp.zeros_like(rows_in)

    mine_local = lax.dynamic_index_in_dim(weights, core, 1, keepdims=False)
    mine = lax.all_gather(mine_local, SHARD, axis=0, tiled=True)
    theirs = lax.ppermute(mine, REP, core_pairs(nrep))

    outputs, input_grads, grad_mine = run_expert(
        mine, inputs, upstream, starts[core], padded[core] // BLOCK, outputs, input_grads
    )
    outputs, input_grads, grad_theirs = run_expert(
        theirs, inputs, upstream, starts[other], padded[other] // BLOCK, outputs, input_grads
    )
    grad_mine = grad_mine + lax.ppermute(grad_theirs, REP, core_pairs(nrep))
    ny, nzh, nx = (lax.axis_size(a) for a in SHARD)
    rows = grad_mine.shape[0] // (ny * nzh * nx)
    part = grad_mine.reshape(ny, nzh, nx, rows, -1).transpose(2, 0, 1, 3, 4)
    part = part.reshape(grad_mine.shape)
    for axis in ("x", "y", "zh"):
        part = lax.psum_scatter(part, axis, scatter_dimension=0, tiled=True)
    part = part + lax.ppermute(part, REP, chip_pairs(nrep))
    part_other = lax.ppermute(part, REP, core_pairs(nrep))
    first = jnp.where(core == 0, part, part_other)
    second = jnp.where(core == 0, part_other, part)
    reduced = jnp.stack([first, second], axis=1)
    return (outputs, input_grads, reduced)


def physical_mesh(mesh):
    devices = np.asarray(mesh.devices)
    flat = devices.reshape(-1)
    nx = len({d.coords[0] for d in flat})
    ny = len({d.coords[1] for d in flat})
    nshard, nrep = mesh.shape["shard"], mesh.shape["rep"]
    shape = (ny, nshard // (nx * ny), nx, nrep // 2, 2)
    return Mesh(devices.reshape(shape), SHARD + REP)


def solution(mesh):
    rows = P(SHARD + REP, None)
    in_specs = (rows, rows, rows, P(SHARD, None, None))
    out_specs = (rows, rows, P(SHARD, None, None))
    return jax.shard_map(
        local, mesh=physical_mesh(mesh), in_specs=in_specs, out_specs=out_specs, check_vma=False
    )
```

```python
import jax
import jax.numpy as jnp
import numpy as np
from jax import lax
from jax.sharding import Mesh
from jax.sharding import PartitionSpec as P

BLOCK = 128


def expert_block(inputs, upstream, expert_slab):
    hidden_width = expert_slab.shape[1] // 3
    gate_up = expert_slab[:, : 2 * hidden_width]
    down_t = expert_slab[:, 2 * hidden_width :]
    project = jnp.dot(inputs, gate_up, preferred_element_type=jnp.float32)
    gate_pre = project[:, :hidden_width]
    up_pre = project[:, hidden_width:]
    gate_sigmoid = jax.nn.sigmoid(gate_pre)
    active = gate_pre * gate_sigmoid
    hidden = (active * up_pre).astype(jnp.bfloat16)
    output = lax.dot_general(
        hidden, down_t, (((1,), (1,)), ((), ())), preferred_element_type=jnp.float32
    ).astype(jnp.bfloat16)
    hidden_grad = jnp.dot(upstream, down_t, preferred_element_type=jnp.float32)
    down_grad = lax.dot_general(
        upstream, hidden, (((0,), (0,)), ((), ())), preferred_element_type=jnp.float32
    )
    gate_grad = hidden_grad * up_pre * gate_sigmoid * (1.0 + gate_pre * (1.0 - gate_sigmoid))
    up_grad = hidden_grad * active
    joint_grad = jnp.concatenate([gate_grad, up_grad], axis=1).astype(jnp.bfloat16)
    proj_grad = lax.dot_general(
        inputs, joint_grad, (((0,), (0,)), ((), ())), preferred_element_type=jnp.float32
    )
    input_grad = lax.dot_general(
        joint_grad, gate_up, (((1,), (1,)), ((), ())), preferred_element_type=jnp.float32
    ).astype(jnp.bfloat16)
    return (output, input_grad, jnp.concatenate([proj_grad, down_grad], axis=1))


def run_expert(expert_slab, inputs, upstream, rows):
    inputs = jnp.where(rows[:, None], inputs, jnp.zeros_like(inputs))
    upstream = jnp.where(rows[:, None], upstream, jnp.zeros_like(upstream))
    return expert_block(inputs, upstream, expert_slab)


SHARD = ("y", "zh", "x")
REP = ("zl", "c")


def core_pairs(n):
    return [(i, i ^ 1) for i in range(n)]


def chip_pairs(n):
    return [(i, i ^ 2) for i in range(n)]


def local(rows_in, cotangent, expert_counts, weights):
    nrep = lax.axis_size(REP)
    core = lax.axis_index("c")
    other = 1 - core
    counts = expert_counts[0]
    padded = (counts + BLOCK - 1) // BLOCK * BLOCK
    starts = jnp.cumsum(padded) - padded
    position = jnp.arange(rows_in.shape[0], dtype=jnp.int32)
    live = (position[:, None] >= starts[None, :]) & (position[:, None] < (starts + counts)[None, :])
    live_mine = jnp.where(core == 0, live[:, 0], live[:, 1])
    live_theirs = jnp.where(core == 0, live[:, 1], live[:, 0])

    mine_local = lax.dynamic_index_in_dim(weights, core, 1, keepdims=False)
    mine = lax.all_gather(mine_local, SHARD, axis=0, tiled=True)
    theirs = lax.ppermute(mine, REP, core_pairs(nrep))

    out_mine, in_grad_mine, grad_mine = run_expert(mine, rows_in, cotangent, live_mine)
    out_theirs, in_grad_theirs, grad_theirs = run_expert(theirs, rows_in, cotangent, live_theirs)
    zero = jnp.zeros_like(rows_in)
    outputs = jnp.where(
        live_mine[:, None], out_mine, jnp.where(live_theirs[:, None], out_theirs, zero)
    )
    input_grads = jnp.where(
        live_mine[:, None], in_grad_mine, jnp.where(live_theirs[:, None], in_grad_theirs, zero)
    )
    ny, nzh, nx = (lax.axis_size(a) for a in SHARD)
    rows = grad_mine.shape[0] // (ny * nzh * nx)
    part = grad_mine + lax.ppermute(grad_theirs, REP, core_pairs(nrep))
    part = part.reshape(ny, nzh, nx, rows, -1).transpose(2, 0, 1, 3, 4)
    part = part.reshape(grad_mine.shape)
    for axis in ("x", "y", "zh"):
        part = lax.psum_scatter(part, axis, scatter_dimension=0, tiled=True)
    part = part + lax.ppermute(part, REP, chip_pairs(nrep))
    part_other = lax.ppermute(part, REP, core_pairs(nrep))
    first = jnp.where(core == 0, part, part_other)
    second = jnp.where(core == 0, part_other, part)
    reduced = jnp.stack([first, second], axis=1)
    return (outputs, input_grads, reduced)


def physical_mesh(mesh):
    devices = np.asarray(mesh.devices)
    flat = devices.reshape(-1)
    nx = len({d.coords[0] for d in flat})
    ny = len({d.coords[1] for d in flat})
    nshard, nrep = mesh.shape["shard"], mesh.shape["rep"]
    shape = (ny, nshard // (nx * ny), nx, nrep // 2, 2)
    return Mesh(devices.reshape(shape), SHARD + REP)


def solution(mesh):
    rows = P(SHARD + REP, None)
    in_specs = (rows, rows, rows, P(SHARD, None, None))
    out_specs = (rows, rows, P(SHARD, None, None))
    return jax.shard_map(
        local, mesh=physical_mesh(mesh), in_specs=in_specs, out_specs=out_specs, check_vma=False
    )
```

```python
import jax
import jax.numpy as jnp
import numpy as np
from jax import lax
from jax.sharding import Mesh
from jax.sharding import PartitionSpec as P

BLOCK = 128


def expert_block(inputs, upstream, expert_slab):
    hidden_width = expert_slab.shape[1] // 3
    gate_up = expert_slab[:, : 2 * hidden_width]
    down_t = expert_slab[:, 2 * hidden_width :]
    project = jnp.dot(inputs, gate_up, preferred_element_type=jnp.float32)
    gate_pre = project[:, :hidden_width]
    up_pre = project[:, hidden_width:]
    gate_sigmoid = jax.nn.sigmoid(gate_pre)
    active = gate_pre * gate_sigmoid
    hidden = (active * up_pre).astype(jnp.bfloat16)
    output = lax.dot_general(
        hidden, down_t, (((1,), (1,)), ((), ())), preferred_element_type=jnp.float32
    ).astype(jnp.bfloat16)
    hidden_grad = jnp.dot(upstream, down_t, preferred_element_type=jnp.float32)
    down_grad = lax.dot_general(
        upstream, hidden, (((0,), (0,)), ((), ())), preferred_element_type=jnp.float32
    )
    gate_grad = hidden_grad * up_pre * gate_sigmoid * (1.0 + gate_pre * (1.0 - gate_sigmoid))
    up_grad = hidden_grad * active
    joint_grad = jnp.concatenate([gate_grad, up_grad], axis=1).astype(jnp.bfloat16)
    proj_grad = lax.dot_general(
        inputs, joint_grad, (((0,), (0,)), ((), ())), preferred_element_type=jnp.float32
    )
    input_grad = lax.dot_general(
        joint_grad, gate_up, (((1,), (1,)), ((), ())), preferred_element_type=jnp.float32
    ).astype(jnp.bfloat16)
    return (output, input_grad, jnp.concatenate([proj_grad, down_grad], axis=1))


def run_expert(expert_slab, inputs, upstream, rows):
    inputs = jnp.where(rows[:, None], inputs, jnp.zeros_like(inputs))
    upstream = jnp.where(rows[:, None], upstream, jnp.zeros_like(upstream))
    return expert_block(inputs, upstream, expert_slab)


SHARD = ("y", "zh", "x")
REP = ("zl", "c")


def core_pairs(n):
    return [(i, i ^ 1) for i in range(n)]


def chip_pairs(n):
    return [(i, i ^ 2) for i in range(n)]


def local(rows_in, cotangent, expert_counts, weights):
    nrep = lax.axis_size(REP)
    core = lax.axis_index("c")
    counts = expert_counts[0]
    padded = (counts + BLOCK - 1) // BLOCK * BLOCK
    starts = jnp.cumsum(padded) - padded
    position = jnp.arange(rows_in.shape[0], dtype=jnp.int32)
    live = (position[:, None] >= starts[None, :]) & (position[:, None] < (starts + counts)[None, :])
    live_mine = jnp.where(core == 0, live[:, 0], live[:, 1])
    live_theirs = jnp.where(core == 0, live[:, 1], live[:, 0])

    mine_local = lax.dynamic_index_in_dim(weights, core, 1, keepdims=False)
    mine = mine_local
    for axis in ("x", "zh", "y"):
        mine = gather_axis(mine, axis)
    theirs = lax.ppermute(mine, REP, core_pairs(nrep))

    out_mine, in_grad_mine, grad_mine = run_expert(mine, rows_in, cotangent, live_mine)
    out_theirs, in_grad_theirs, grad_theirs = run_expert(theirs, rows_in, cotangent, live_theirs)
    zero = jnp.zeros_like(rows_in)
    outputs = jnp.where(
        live_mine[:, None], out_mine, jnp.where(live_theirs[:, None], out_theirs, zero)
    )
    input_grads = jnp.where(
        live_mine[:, None], in_grad_mine, jnp.where(live_theirs[:, None], in_grad_theirs, zero)
    )
    ny, nzh, nx = (lax.axis_size(a) for a in SHARD)
    rows = grad_mine.shape[0] // (ny * nzh * nx)
    part = grad_mine + lax.ppermute(grad_theirs, REP, core_pairs(nrep))
    part = part.reshape(ny, nzh, nx, rows, -1).transpose(2, 0, 1, 3, 4)
    part = part.reshape(grad_mine.shape)
    for axis in ("x", "y", "zh"):
        part = scatter_axis(part, axis)
    part = part + lax.ppermute(part, REP, chip_pairs(nrep))
    part_other = lax.ppermute(part, REP, core_pairs(nrep))
    first = jnp.where(core == 0, part, part_other)
    second = jnp.where(core == 0, part_other, part)
    reduced = jnp.stack([first, second], axis=1)
    return (outputs, input_grads, reduced)


def shift_pairs(n, k):
    return [(j, (j + k) % n) for j in range(n)]


def gather_axis(a, axis):
    n = lax.axis_size(axis)
    i = lax.axis_index(axis)
    rows = a.shape[0]
    out = jnp.zeros((n * rows,) + a.shape[1:], a.dtype)
    out = lax.dynamic_update_slice_in_dim(out, a, i * rows, 0)
    for k in range(1, n):
        got = lax.ppermute(a, axis, shift_pairs(n, k))
        out = lax.dynamic_update_slice_in_dim(out, got, ((i - k) % n) * rows, 0)
    return out


def scatter_axis(a, axis):
    n = lax.axis_size(axis)
    i = lax.axis_index(axis)
    rows = a.shape[0] // n
    total = lax.dynamic_slice_in_dim(a, i * rows, rows, 0)
    for k in range(1, n):
        chunk = lax.dynamic_slice_in_dim(a, ((i + k) % n) * rows, rows, 0)
        total = total + lax.ppermute(chunk, axis, shift_pairs(n, k))
    return total


def physical_mesh(mesh):
    devices = np.asarray(mesh.devices)
    flat = devices.reshape(-1)
    nx = len({d.coords[0] for d in flat})
    ny = len({d.coords[1] for d in flat})
    nshard, nrep = mesh.shape["shard"], mesh.shape["rep"]
    shape = (ny, nshard // (nx * ny), nx, nrep // 2, 2)
    return Mesh(devices.reshape(shape), SHARD + REP)


def solution(mesh):
    rows = P(SHARD + REP, None)
    in_specs = (rows, rows, rows, P(SHARD, None, None))
    out_specs = (rows, rows, P(SHARD, None, None))
    return jax.shard_map(
        local, mesh=physical_mesh(mesh), in_specs=in_specs, out_specs=out_specs, check_vma=False
    )
```

```python
import jax
import jax.numpy as jnp
import numpy as np
from jax import lax
from jax.sharding import Mesh
from jax.sharding import PartitionSpec as P

BLOCK = 128


def expert_block(inputs, upstream, expert_slab):
    hidden_width = expert_slab.shape[1] // 3
    gate_up = expert_slab[:, : 2 * hidden_width]
    down_t = expert_slab[:, 2 * hidden_width :]
    project = jnp.dot(inputs, gate_up, preferred_element_type=jnp.float32)
    gate_pre = project[:, :hidden_width]
    up_pre = project[:, hidden_width:]
    gate_sigmoid = jax.nn.sigmoid(gate_pre)
    active = gate_pre * gate_sigmoid
    hidden = (active * up_pre).astype(jnp.bfloat16)
    output = lax.dot_general(
        hidden, down_t, (((1,), (1,)), ((), ())), preferred_element_type=jnp.float32
    ).astype(jnp.bfloat16)
    hidden_grad = jnp.dot(upstream, down_t, preferred_element_type=jnp.float32)
    down_grad = lax.dot_general(
        upstream, hidden, (((0,), (0,)), ((), ())), preferred_element_type=jnp.float32
    )
    gate_grad = hidden_grad * up_pre * gate_sigmoid * (1.0 + gate_pre * (1.0 - gate_sigmoid))
    up_grad = hidden_grad * active
    joint_grad = jnp.concatenate([gate_grad, up_grad], axis=1).astype(jnp.bfloat16)
    proj_grad = lax.dot_general(
        inputs, joint_grad, (((0,), (0,)), ((), ())), preferred_element_type=jnp.float32
    )
    input_grad = lax.dot_general(
        joint_grad, gate_up, (((1,), (1,)), ((), ())), preferred_element_type=jnp.float32
    ).astype(jnp.bfloat16)
    return (output, input_grad, jnp.concatenate([proj_grad, down_grad], axis=1))


def run_expert(expert_slab, inputs, upstream, rows):
    inputs = jnp.where(rows[:, None], inputs, jnp.zeros_like(inputs))
    upstream = jnp.where(rows[:, None], upstream, jnp.zeros_like(upstream))
    return expert_block(inputs, upstream, expert_slab)


SHARD = ("y", "zh", "x")
REP = ("zl", "c")


def core_pairs(n):
    return [(i, i ^ 1) for i in range(n)]


def chip_pairs(n):
    return [(i, i ^ 2) for i in range(n)]


def local(rows_in, cotangent, expert_counts, weights):
    nrep = lax.axis_size(REP)
    core = lax.axis_index("c")
    counts = expert_counts[0]
    padded = (counts + BLOCK - 1) // BLOCK * BLOCK
    starts = jnp.cumsum(padded) - padded
    position = jnp.arange(rows_in.shape[0], dtype=jnp.int32)
    live = (position[:, None] >= starts[None, :]) & (position[:, None] < (starts + counts)[None, :])
    live_mine = jnp.where(core == 0, live[:, 0], live[:, 1])
    live_theirs = jnp.where(core == 0, live[:, 1], live[:, 0])

    mine_local = lax.dynamic_index_in_dim(weights, core, 1, keepdims=False)
    ny, nzh, nx = (lax.axis_size(a) for a in SHARD)
    half = mine_local.shape[0] // 2
    first_half = mine_local[:half]
    for axis in ("x", "zh", "y"):
        first_half = gather_axis(first_half, axis)
    second_half = mine_local[half:]
    for axis in ("y", "zh", "x"):
        second_half = gather_axis(second_half, axis)
    first_half = first_half.reshape(ny, nzh, nx, half, -1)
    second_half = second_half.reshape(nx, nzh, ny, half, -1).transpose(2, 1, 0, 3, 4)
    mine = jnp.stack([first_half, second_half], axis=3).reshape(-1, mine_local.shape[1])
    theirs = lax.ppermute(mine, REP, core_pairs(nrep))

    out_mine, in_grad_mine, grad_mine = run_expert(mine, rows_in, cotangent, live_mine)
    out_theirs, in_grad_theirs, grad_theirs = run_expert(theirs, rows_in, cotangent, live_theirs)
    zero = jnp.zeros_like(rows_in)
    outputs = jnp.where(
        live_mine[:, None], out_mine, jnp.where(live_theirs[:, None], out_theirs, zero)
    )
    input_grads = jnp.where(
        live_mine[:, None], in_grad_mine, jnp.where(live_theirs[:, None], in_grad_theirs, zero)
    )
    part = grad_mine + lax.ppermute(grad_theirs, REP, core_pairs(nrep))
    part = part.reshape(ny, nzh, nx, 2, half, -1)
    cols = part.shape[-1]
    first_half = part[:, :, :, 0].transpose(2, 0, 1, 3, 4).reshape(-1, cols)
    second_half = part[:, :, :, 1].transpose(0, 2, 1, 3, 4).reshape(-1, cols)
    first_half = scatter_axis(first_half, "x", jnp.bfloat16)
    second_half = scatter_axis(second_half, "y", jnp.bfloat16)
    first_half = scatter_axis(scatter_axis(first_half, "y"), "zh")
    second_half = scatter_axis(scatter_axis(second_half, "x"), "zh")
    part = jnp.concatenate([first_half, second_half], axis=0)
    part = part + lax.ppermute(part, REP, chip_pairs(nrep))
    part_other = lax.ppermute(part, REP, core_pairs(nrep))
    first = jnp.where(core == 0, part, part_other)
    second = jnp.where(core == 0, part_other, part)
    reduced = jnp.stack([first, second], axis=1)
    return (outputs, input_grads, reduced)


def shift_pairs(n, k):
    return [(j, (j + k) % n) for j in range(n)]


def gather_axis(a, axis):
    n = lax.axis_size(axis)
    i = lax.axis_index(axis)
    rows = a.shape[0]
    out = jnp.zeros((n * rows,) + a.shape[1:], a.dtype)
    out = lax.dynamic_update_slice_in_dim(out, a, i * rows, 0)
    for k in range(1, n):
        got = lax.ppermute(a, axis, shift_pairs(n, k))
        out = lax.dynamic_update_slice_in_dim(out, got, ((i - k) % n) * rows, 0)
    return out


def scatter_axis(a, axis, wire=None):
    n = lax.axis_size(axis)
    i = lax.axis_index(axis)
    rows = a.shape[0] // n
    total = lax.dynamic_slice_in_dim(a, i * rows, rows, 0)
    for k in range(1, n):
        chunk = lax.dynamic_slice_in_dim(a, ((i + k) % n) * rows, rows, 0)
        if wire is not None:
            chunk = chunk.astype(wire)
        total = total + lax.ppermute(chunk, axis, shift_pairs(n, k)).astype(total.dtype)
    return total


def physical_mesh(mesh):
    devices = np.asarray(mesh.devices)
    flat = devices.reshape(-1)
    nx = len({d.coords[0] for d in flat})
    ny = len({d.coords[1] for d in flat})
    nshard, nrep = mesh.shape["shard"], mesh.shape["rep"]
    shape = (ny, nshard // (nx * ny), nx, nrep // 2, 2)
    return Mesh(devices.reshape(shape), SHARD + REP)


def solution(mesh):
    rows = P(SHARD + REP, None)
    in_specs = (rows, rows, rows, P(SHARD, None, None))
    out_specs = (rows, rows, P(SHARD, None, None))
    return jax.shard_map(
        local, mesh=physical_mesh(mesh), in_specs=in_specs, out_specs=out_specs, check_vma=False
    )
```

```python
import jax
import jax.numpy as jnp
import numpy as np
from jax import lax
from jax.sharding import Mesh
from jax.sharding import PartitionSpec as P

BLOCK = 128


def expert_block(inputs, upstream, expert_slab, inputs_t, upstream_t):
    hidden_width = expert_slab.shape[1] // 3
    gate_up = expert_slab[:, : 2 * hidden_width]
    down_t = expert_slab[:, 2 * hidden_width :]
    project = jnp.dot(inputs, gate_up, preferred_element_type=jnp.float32)
    gate_pre = project[:, :hidden_width]
    up_pre = project[:, hidden_width:]
    gate_sigmoid = jax.nn.sigmoid(gate_pre)
    active = gate_pre * gate_sigmoid
    hidden = (active * up_pre).astype(jnp.bfloat16)
    output = lax.dot_general(
        hidden, down_t, (((1,), (1,)), ((), ())), preferred_element_type=jnp.float32
    ).astype(jnp.bfloat16)
    hidden_grad = jnp.dot(upstream, down_t, preferred_element_type=jnp.float32)
    down_grad = lax.dot_general(
        upstream_t, hidden, (((0,), (0,)), ((), ())), preferred_element_type=jnp.float32
    )
    gate_grad = hidden_grad * up_pre * gate_sigmoid * (1.0 + gate_pre * (1.0 - gate_sigmoid))
    up_grad = hidden_grad * active
    joint_grad = jnp.concatenate([gate_grad, up_grad], axis=1).astype(jnp.bfloat16)
    proj_grad = lax.dot_general(
        inputs_t, joint_grad, (((0,), (0,)), ((), ())), preferred_element_type=jnp.float32
    )
    input_grad = lax.dot_general(
        joint_grad, gate_up, (((1,), (1,)), ((), ())), preferred_element_type=jnp.float32
    ).astype(jnp.bfloat16)
    return (output, input_grad, jnp.concatenate([proj_grad, down_grad], axis=1))


def run_expert(expert_slab, inputs, upstream, rows, reorder):
    inputs = jnp.where(rows[:, None], inputs, jnp.zeros_like(inputs))
    upstream = jnp.where(rows[:, None], upstream, jnp.zeros_like(upstream))
    return expert_block(inputs, upstream, expert_slab, reorder(inputs), reorder(upstream))


SHARD = ("y", "zh", "x")
REP = ("zl", "c")


def core_pairs(n):
    return [(i, i ^ 1) for i in range(n)]


def chip_pairs(n):
    return [(i, i ^ 2) for i in range(n)]


def local(rows_in, cotangent, expert_counts, weights):
    nrep = lax.axis_size(REP)
    core = lax.axis_index("c")
    counts = expert_counts[0]
    padded = (counts + BLOCK - 1) // BLOCK * BLOCK
    starts = jnp.cumsum(padded) - padded
    position = jnp.arange(rows_in.shape[0], dtype=jnp.int32)
    live = (position[:, None] >= starts[None, :]) & (position[:, None] < (starts + counts)[None, :])
    live_mine = jnp.where(core == 0, live[:, 0], live[:, 1])
    live_theirs = jnp.where(core == 0, live[:, 1], live[:, 0])

    mine_local = lax.dynamic_index_in_dim(weights, core, 1, keepdims=False)
    ny, nzh, nx = (lax.axis_size(a) for a in SHARD)
    half = mine_local.shape[0] // 2
    first_half = mine_local[:half]
    for axis in ("x", "zh", "y"):
        first_half = gather_axis(first_half, axis)
    second_half = mine_local[half:]
    for axis in ("y", "zh", "x"):
        second_half = gather_axis(second_half, axis)
    first_half = first_half.reshape(ny, nzh, nx, half, -1)
    second_half = second_half.reshape(nx, nzh, ny, half, -1).transpose(2, 1, 0, 3, 4)
    mine = jnp.stack([first_half, second_half], axis=3).reshape(-1, mine_local.shape[1])
    theirs = lax.ppermute(mine, REP, core_pairs(nrep))

    def reorder(a):
        g = a.reshape(a.shape[0], ny, nzh, nx, 2, half)
        first = g[:, :, :, :, 0].transpose(0, 3, 1, 2, 4).reshape(a.shape[0], -1)
        second = g[:, :, :, :, 1].transpose(0, 1, 3, 2, 4).reshape(a.shape[0], -1)
        return jnp.concatenate([first, second], axis=1)

    out_mine, in_grad_mine, grad_mine = run_expert(mine, rows_in, cotangent, live_mine, reorder)
    out_theirs, in_grad_theirs, grad_theirs = run_expert(
        theirs, rows_in, cotangent, live_theirs, reorder
    )
    zero = jnp.zeros_like(rows_in)
    outputs = jnp.where(
        live_mine[:, None], out_mine, jnp.where(live_theirs[:, None], out_theirs, zero)
    )
    input_grads = jnp.where(
        live_mine[:, None], in_grad_mine, jnp.where(live_theirs[:, None], in_grad_theirs, zero)
    )
    part = grad_mine + lax.ppermute(grad_theirs, REP, core_pairs(nrep))
    first_half, second_half = jnp.split(part, 2, axis=0)
    first_half = scatter_axis(first_half, "x", jnp.bfloat16)
    second_half = scatter_axis(second_half, "y", jnp.bfloat16)
    first_half, second_half, outputs, input_grads = lax.optimization_barrier(
        (first_half, second_half, outputs, input_grads)
    )
    first_half = scatter_axis(scatter_axis(first_half, "y"), "zh")
    second_half = scatter_axis(scatter_axis(second_half, "x"), "zh")
    part = jnp.concatenate([first_half, second_half], axis=0)
    part = part + lax.ppermute(part, REP, chip_pairs(nrep))
    part_other = lax.ppermute(part, REP, core_pairs(nrep))
    first = jnp.where(core == 0, part, part_other)
    second = jnp.where(core == 0, part_other, part)
    reduced = jnp.stack([first, second], axis=1)
    return (outputs, input_grads, reduced)


def shift_pairs(n, k):
    return [(j, (j + k) % n) for j in range(n)]


def gather_axis(a, axis):
    n = lax.axis_size(axis)
    i = lax.axis_index(axis)
    rows = a.shape[0]
    out = jnp.zeros((n * rows,) + a.shape[1:], a.dtype)
    out = lax.dynamic_update_slice_in_dim(out, a, i * rows, 0)
    for k in range(1, n):
        got = lax.ppermute(a, axis, shift_pairs(n, k))
        out = lax.dynamic_update_slice_in_dim(out, got, ((i - k) % n) * rows, 0)
    return out


def scatter_axis(a, axis, wire=None):
    n = lax.axis_size(axis)
    i = lax.axis_index(axis)
    rows = a.shape[0] // n
    total = lax.dynamic_slice_in_dim(a, i * rows, rows, 0)
    for k in range(1, n):
        chunk = lax.dynamic_slice_in_dim(a, ((i + k) % n) * rows, rows, 0)
        if wire is not None:
            chunk = chunk.astype(wire)
        total = total + lax.ppermute(chunk, axis, shift_pairs(n, k)).astype(total.dtype)
    return total


def physical_mesh(mesh):
    devices = np.asarray(mesh.devices)
    flat = devices.reshape(-1)
    nx = len({d.coords[0] for d in flat})
    ny = len({d.coords[1] for d in flat})
    nshard, nrep = mesh.shape["shard"], mesh.shape["rep"]
    shape = (ny, nshard // (nx * ny), nx, nrep // 2, 2)
    return Mesh(devices.reshape(shape), SHARD + REP)


def solution(mesh):
    rows = P(SHARD + REP, None)
    in_specs = (rows, rows, rows, P(SHARD, None, None))
    out_specs = (rows, rows, P(SHARD, None, None))
    return jax.shard_map(
        local, mesh=physical_mesh(mesh), in_specs=in_specs, out_specs=out_specs, check_vma=False
    )
```

```python
import jax
import jax.numpy as jnp
import numpy as np
from jax import lax
from jax.sharding import Mesh
from jax.sharding import PartitionSpec as P

BLOCK = 128


def expert_block(inputs, upstream, expert_slab):
    hidden_width = expert_slab.shape[1] // 3
    gate_up = expert_slab[:, : 2 * hidden_width]
    down_t = expert_slab[:, 2 * hidden_width :]
    project = jnp.dot(inputs, gate_up, preferred_element_type=jnp.float32)
    gate_pre = project[:, :hidden_width]
    up_pre = project[:, hidden_width:]
    gate_sigmoid = jax.nn.sigmoid(gate_pre)
    active = gate_pre * gate_sigmoid
    hidden = (active * up_pre).astype(jnp.bfloat16)
    output = lax.dot_general(
        hidden, down_t, (((1,), (1,)), ((), ())), preferred_element_type=jnp.float32
    ).astype(jnp.bfloat16)
    hidden_grad = jnp.dot(upstream, down_t, preferred_element_type=jnp.float32)
    down_grad = lax.dot_general(
        upstream, hidden, (((0,), (0,)), ((), ())), preferred_element_type=jnp.float32
    )
    gate_grad = hidden_grad * up_pre * gate_sigmoid * (1.0 + gate_pre * (1.0 - gate_sigmoid))
    up_grad = hidden_grad * active
    joint_grad = jnp.concatenate([gate_grad, up_grad], axis=1).astype(jnp.bfloat16)
    proj_grad = lax.dot_general(
        inputs, joint_grad, (((0,), (0,)), ((), ())), preferred_element_type=jnp.float32
    )
    input_grad = lax.dot_general(
        joint_grad, gate_up, (((1,), (1,)), ((), ())), preferred_element_type=jnp.float32
    ).astype(jnp.bfloat16)
    return (output, input_grad, jnp.concatenate([proj_grad, down_grad], axis=1))


def run_expert(expert_slab, inputs, upstream, rows):
    inputs = jnp.where(rows[:, None], inputs, jnp.zeros_like(inputs))
    upstream = jnp.where(rows[:, None], upstream, jnp.zeros_like(upstream))
    return expert_block(inputs, upstream, expert_slab)


SHARD = ("y", "zh", "x")
REP = ("zl", "c")


def core_pairs(n):
    return [(i, i ^ 1) for i in range(n)]


def chip_pairs(n):
    return [(i, i ^ 2) for i in range(n)]


def local(rows_in, cotangent, expert_counts, weights):
    nrep = lax.axis_size(REP)
    core = lax.axis_index("c")
    counts = expert_counts[0]
    padded = (counts + BLOCK - 1) // BLOCK * BLOCK
    starts = jnp.cumsum(padded) - padded
    position = jnp.arange(rows_in.shape[0], dtype=jnp.int32)
    live = (position[:, None] >= starts[None, :]) & (position[:, None] < (starts + counts)[None, :])
    live_mine = jnp.where(core == 0, live[:, 0], live[:, 1])
    live_theirs = jnp.where(core == 0, live[:, 1], live[:, 0])

    mine_local = lax.dynamic_index_in_dim(weights, core, 1, keepdims=False)
    ny, nzh, nx = (lax.axis_size(a) for a in SHARD)
    half = mine_local.shape[0] // 2
    first_half = mine_local[:half]
    for axis in ("zh", "x", "y"):
        first_half = gather_axis(first_half, axis)
    second_half = mine_local[half:]
    for axis in ("zh", "y", "x"):
        second_half = gather_axis(second_half, axis)
    first_half = first_half.reshape(ny, nx, nzh, half, -1).transpose(0, 2, 1, 3, 4)
    second_half = second_half.reshape(nx, ny, nzh, half, -1).transpose(1, 2, 0, 3, 4)
    mine = jnp.stack([first_half, second_half], axis=3).reshape(-1, mine_local.shape[1])
    theirs = lax.ppermute(mine, REP, core_pairs(nrep))

    out_mine, in_grad_mine, grad_mine = run_expert(mine, rows_in, cotangent, live_mine)
    out_theirs, in_grad_theirs, grad_theirs = run_expert(theirs, rows_in, cotangent, live_theirs)
    zero = jnp.zeros_like(rows_in)
    outputs = jnp.where(
        live_mine[:, None], out_mine, jnp.where(live_theirs[:, None], out_theirs, zero)
    )
    input_grads = jnp.where(
        live_mine[:, None], in_grad_mine, jnp.where(live_theirs[:, None], in_grad_theirs, zero)
    )
    part = grad_mine + lax.ppermute(grad_theirs, REP, core_pairs(nrep))
    part = part.reshape(ny, nzh, nx, 2, half, -1)
    cols = part.shape[-1]
    first_half = part[:, :, :, 0].transpose(2, 0, 1, 3, 4).reshape(-1, cols)
    second_half = part[:, :, :, 1].transpose(0, 2, 1, 3, 4).reshape(-1, cols)
    first_half = scatter_axis(first_half, "x", jnp.bfloat16)
    second_half = scatter_axis(second_half, "y", jnp.bfloat16)
    first_half = scatter_axis(scatter_axis(first_half, "y"), "zh")
    second_half = scatter_axis(scatter_axis(second_half, "x"), "zh")
    part = jnp.concatenate([first_half, second_half], axis=0)
    part = part + lax.ppermute(part, REP, chip_pairs(nrep))
    part_other = lax.ppermute(part, REP, core_pairs(nrep))
    first = jnp.where(core == 0, part, part_other)
    second = jnp.where(core == 0, part_other, part)
    reduced = jnp.stack([first, second], axis=1)
    return (outputs, input_grads, reduced)


def shift_pairs(n, k):
    return [(j, (j + k) % n) for j in range(n)]


def gather_axis(a, axis):
    n = lax.axis_size(axis)
    i = lax.axis_index(axis)
    rows = a.shape[0]
    out = jnp.zeros((n * rows,) + a.shape[1:], a.dtype)
    out = lax.dynamic_update_slice_in_dim(out, a, i * rows, 0)
    for k in range(1, n):
        got = lax.ppermute(a, axis, shift_pairs(n, k))
        out = lax.dynamic_update_slice_in_dim(out, got, ((i - k) % n) * rows, 0)
    return out


def scatter_axis(a, axis, wire=None):
    n = lax.axis_size(axis)
    i = lax.axis_index(axis)
    rows = a.shape[0] // n
    total = lax.dynamic_slice_in_dim(a, i * rows, rows, 0)
    for k in range(1, n):
        chunk = lax.dynamic_slice_in_dim(a, ((i + k) % n) * rows, rows, 0)
        if wire is not None:
            chunk = chunk.astype(wire)
        total = total + lax.ppermute(chunk, axis, shift_pairs(n, k)).astype(total.dtype)
    return total


def physical_mesh(mesh):
    devices = np.asarray(mesh.devices)
    flat = devices.reshape(-1)
    nx = len({d.coords[0] for d in flat})
    ny = len({d.coords[1] for d in flat})
    nshard, nrep = mesh.shape["shard"], mesh.shape["rep"]
    shape = (ny, nshard // (nx * ny), nx, nrep // 2, 2)
    return Mesh(devices.reshape(shape), SHARD + REP)


def solution(mesh):
    rows = P(SHARD + REP, None)
    in_specs = (rows, rows, rows, P(SHARD, None, None))
    out_specs = (rows, rows, P(SHARD, None, None))
    return jax.shard_map(
        local, mesh=physical_mesh(mesh), in_specs=in_specs, out_specs=out_specs, check_vma=False
    )
```

```python
import jax
import jax.numpy as jnp
import numpy as np
from jax import lax
from jax.sharding import Mesh
from jax.sharding import PartitionSpec as P

BLOCK = 128


def expert_block(inputs, upstream, expert_slab):
    hidden_width = expert_slab.shape[1] // 3
    gate_up = expert_slab[:, : 2 * hidden_width]
    down_t = expert_slab[:, 2 * hidden_width :]
    project = jnp.dot(inputs, gate_up, preferred_element_type=jnp.float32)
    gate_pre = project[:, :hidden_width]
    up_pre = project[:, hidden_width:]
    gate_sigmoid = jax.nn.sigmoid(gate_pre)
    active = gate_pre * gate_sigmoid
    hidden = (active * up_pre).astype(jnp.bfloat16)
    output = lax.dot_general(
        hidden, down_t, (((1,), (1,)), ((), ())), preferred_element_type=jnp.float32
    ).astype(jnp.bfloat16)
    hidden_grad = jnp.dot(upstream, down_t, preferred_element_type=jnp.float32)
    down_grad = lax.dot_general(
        upstream, hidden, (((0,), (0,)), ((), ())), preferred_element_type=jnp.float32
    )
    gate_grad = hidden_grad * up_pre * gate_sigmoid * (1.0 + gate_pre * (1.0 - gate_sigmoid))
    up_grad = hidden_grad * active
    joint_grad = jnp.concatenate([gate_grad, up_grad], axis=1).astype(jnp.bfloat16)
    proj_grad = lax.dot_general(
        inputs, joint_grad, (((0,), (0,)), ((), ())), preferred_element_type=jnp.float32
    )
    input_grad = lax.dot_general(
        joint_grad, gate_up, (((1,), (1,)), ((), ())), preferred_element_type=jnp.float32
    ).astype(jnp.bfloat16)
    return (output, input_grad, jnp.concatenate([proj_grad, down_grad], axis=1))


def run_expert(expert_slab, inputs, upstream, rows):
    inputs = jnp.where(rows[:, None], inputs, jnp.zeros_like(inputs))
    upstream = jnp.where(rows[:, None], upstream, jnp.zeros_like(upstream))
    return expert_block(inputs, upstream, expert_slab)


SHARD = ("y", "zh", "x")
REP = ("zl", "c")


def core_pairs(n):
    return [(i, i ^ 1) for i in range(n)]


def chip_pairs(n):
    return [(i, i ^ 2) for i in range(n)]


def local(rows_in, cotangent, expert_counts, weights):
    nrep = lax.axis_size(REP)
    core = lax.axis_index("c")
    counts = expert_counts[0]
    padded = (counts + BLOCK - 1) // BLOCK * BLOCK
    starts = jnp.cumsum(padded) - padded
    position = jnp.arange(rows_in.shape[0], dtype=jnp.int32)
    live = (position[:, None] >= starts[None, :]) & (position[:, None] < (starts + counts)[None, :])
    live_mine = jnp.where(core == 0, live[:, 0], live[:, 1])
    live_theirs = jnp.where(core == 0, live[:, 1], live[:, 0])

    mine_local = lax.dynamic_index_in_dim(weights, core, 1, keepdims=False)
    ny, nzh, nx = (lax.axis_size(a) for a in SHARD)
    half = mine_local.shape[0] // 2
    first_half = mine_local[:half]
    for axis in ("zh", "x", "y"):
        first_half = gather_axis(first_half, axis)
    second_half = mine_local[half:]
    for axis in ("zh", "y", "x"):
        second_half = gather_axis(second_half, axis)
    first_half = first_half.reshape(ny, nx, nzh, half, -1).transpose(0, 2, 1, 3, 4)
    second_half = second_half.reshape(nx, ny, nzh, half, -1).transpose(1, 2, 0, 3, 4)
    mine = jnp.stack([first_half, second_half], axis=3).reshape(-1, mine_local.shape[1])
    theirs = lax.ppermute(mine, REP, core_pairs(nrep))

    out_mine, in_grad_mine, grad_mine = run_expert(mine, rows_in, cotangent, live_mine)
    out_theirs, in_grad_theirs, grad_theirs = run_expert(theirs, rows_in, cotangent, live_theirs)
    zero = jnp.zeros_like(rows_in)
    outputs = jnp.where(
        live_mine[:, None], out_mine, jnp.where(live_theirs[:, None], out_theirs, zero)
    )
    input_grads = jnp.where(
        live_mine[:, None], in_grad_mine, jnp.where(live_theirs[:, None], in_grad_theirs, zero)
    )
    part = grad_mine + lax.ppermute(grad_theirs, REP, core_pairs(nrep))
    part = part.reshape(ny, nzh, nx, 2, half, -1)
    first_half = scatter_axis(part[:, :, :, 0], "x", 2, jnp.bfloat16)
    second_half = scatter_axis(part[:, :, :, 1], "y", 0, jnp.bfloat16)
    first_half = scatter_axis(scatter_axis(first_half, "y", 0), "zh", 0)
    second_half = scatter_axis(scatter_axis(second_half, "x", 1), "zh", 0)
    part = jnp.concatenate([first_half, second_half], axis=0)
    part = part + lax.ppermute(part, REP, chip_pairs(nrep))
    part_other = lax.ppermute(part, REP, core_pairs(nrep))
    first = jnp.where(core == 0, part, part_other)
    second = jnp.where(core == 0, part_other, part)
    reduced = jnp.stack([first, second], axis=1)
    return (outputs, input_grads, reduced)


def shift_pairs(n, k):
    return [(j, (j + k) % n) for j in range(n)]


def gather_axis(a, axis):
    n = lax.axis_size(axis)
    i = lax.axis_index(axis)
    rows = a.shape[0]
    out = jnp.zeros((n * rows,) + a.shape[1:], a.dtype)
    out = lax.dynamic_update_slice_in_dim(out, a, i * rows, 0)
    for k in range(1, n):
        got = lax.ppermute(a, axis, shift_pairs(n, k))
        out = lax.dynamic_update_slice_in_dim(out, got, ((i - k) % n) * rows, 0)
    return out


def scatter_axis(a, axis, dim=0, wire=None):
    n = lax.axis_size(axis)
    i = lax.axis_index(axis)
    total = lax.dynamic_index_in_dim(a, i, dim, keepdims=False)
    for k in range(1, n):
        chunk = lax.dynamic_index_in_dim(a, (i + k) % n, dim, keepdims=False)
        if wire is not None:
            chunk = chunk.astype(wire)
        total = total + lax.ppermute(chunk, axis, shift_pairs(n, k)).astype(total.dtype)
    return total


def physical_mesh(mesh):
    devices = np.asarray(mesh.devices)
    flat = devices.reshape(-1)
    nx = len({d.coords[0] for d in flat})
    ny = len({d.coords[1] for d in flat})
    nshard, nrep = mesh.shape["shard"], mesh.shape["rep"]
    shape = (ny, nshard // (nx * ny), nx, nrep // 2, 2)
    return Mesh(devices.reshape(shape), SHARD + REP)


def solution(mesh):
    rows = P(SHARD + REP, None)
    in_specs = (rows, rows, rows, P(SHARD, None, None))
    out_specs = (rows, rows, P(SHARD, None, None))
    return jax.shard_map(
        local, mesh=physical_mesh(mesh), in_specs=in_specs, out_specs=out_specs, check_vma=False
    )
```

```python
import jax
import jax.numpy as jnp
import numpy as np
from jax import lax
from jax.sharding import Mesh
from jax.sharding import PartitionSpec as P

BLOCK = 128


def expert_block(inputs, upstream, expert_slab):
    hidden_width = expert_slab.shape[1] // 3
    gate_up = expert_slab[:, : 2 * hidden_width]
    down_t = expert_slab[:, 2 * hidden_width :]
    project = jnp.dot(inputs, gate_up, preferred_element_type=jnp.float32)
    gate_pre = project[:, :hidden_width]
    up_pre = project[:, hidden_width:]
    gate_sigmoid = jax.nn.sigmoid(gate_pre)
    active = gate_pre * gate_sigmoid
    hidden = (active * up_pre).astype(jnp.bfloat16)
    output = lax.dot_general(
        hidden, down_t, (((1,), (1,)), ((), ())), preferred_element_type=jnp.float32
    ).astype(jnp.bfloat16)
    hidden_grad = jnp.dot(upstream, down_t, preferred_element_type=jnp.float32)
    down_grad = lax.dot_general(
        upstream, hidden, (((0,), (0,)), ((), ())), preferred_element_type=jnp.float32
    )
    gate_grad = hidden_grad * up_pre * gate_sigmoid * (1.0 + gate_pre * (1.0 - gate_sigmoid))
    up_grad = hidden_grad * active
    joint_grad = jnp.concatenate([gate_grad, up_grad], axis=1).astype(jnp.bfloat16)
    proj_grad = lax.dot_general(
        inputs, joint_grad, (((0,), (0,)), ((), ())), preferred_element_type=jnp.float32
    )
    input_grad = lax.dot_general(
        joint_grad, gate_up, (((1,), (1,)), ((), ())), preferred_element_type=jnp.float32
    ).astype(jnp.bfloat16)
    return (output, input_grad, jnp.concatenate([proj_grad, down_grad], axis=1))


def run_expert(expert_slab, inputs, upstream, rows):
    inputs = jnp.where(rows[:, None], inputs, jnp.zeros_like(inputs))
    upstream = jnp.where(rows[:, None], upstream, jnp.zeros_like(upstream))
    return expert_block(inputs, upstream, expert_slab)


SHARD = ("y", "zh", "x")
REP = ("zl", "c")


def core_pairs(n):
    return [(i, i ^ 1) for i in range(n)]


def chip_pairs(n):
    return [(i, i ^ 2) for i in range(n)]


def local(rows_in, cotangent, expert_counts, weights):
    nrep = lax.axis_size(REP)
    core = lax.axis_index("c")
    counts = expert_counts[0]
    padded = (counts + BLOCK - 1) // BLOCK * BLOCK
    starts = jnp.cumsum(padded) - padded
    position = jnp.arange(rows_in.shape[0], dtype=jnp.int32)
    live = (position[:, None] >= starts[None, :]) & (position[:, None] < (starts + counts)[None, :])
    live_mine = jnp.where(core == 0, live[:, 0], live[:, 1])
    live_theirs = jnp.where(core == 0, live[:, 1], live[:, 0])

    mine_local = lax.dynamic_index_in_dim(weights, core, 1, keepdims=False)
    ny, nzh, nx = (lax.axis_size(a) for a in SHARD)
    half = mine_local.shape[0] // 2
    first_half = mine_local[:half]
    for axis in ("zh", "x", "y"):
        first_half = gather_axis(first_half, axis)
    second_half = mine_local[half:]
    for axis in ("zh", "y", "x"):
        second_half = gather_axis(second_half, axis)
    first_half = first_half.reshape(ny, nx, nzh, half, -1).transpose(0, 2, 1, 3, 4)
    second_half = second_half.reshape(nx, ny, nzh, half, -1).transpose(1, 2, 0, 3, 4)
    mine = jnp.stack([first_half, second_half], axis=3).reshape(-1, mine_local.shape[1])
    theirs = lax.ppermute(mine, REP, core_pairs(nrep))

    out_mine, in_grad_mine, grad_mine = run_expert(mine, rows_in, cotangent, live_mine)
    out_theirs, in_grad_theirs, grad_theirs = run_expert(theirs, rows_in, cotangent, live_theirs)
    zero = jnp.zeros_like(rows_in)
    outputs = jnp.where(
        live_mine[:, None], out_mine, jnp.where(live_theirs[:, None], out_theirs, zero)
    )
    input_grads = jnp.where(
        live_mine[:, None], in_grad_mine, jnp.where(live_theirs[:, None], in_grad_theirs, zero)
    )
    part = grad_mine + lax.ppermute(grad_theirs, REP, core_pairs(nrep))
    part = part.astype(jnp.bfloat16).reshape(ny, nzh, nx, 2, half, -1)
    first_half = scatter_axis(part[:, :, :, 0], "x", 2)
    second_half = scatter_axis(part[:, :, :, 1], "y", 0)
    first_half = scatter_axis(scatter_axis(first_half, "y", 0), "zh", 0)
    second_half = scatter_axis(scatter_axis(second_half, "x", 1), "zh", 0)
    part = jnp.concatenate([first_half, second_half], axis=0)
    part = part + lax.ppermute(part, REP, chip_pairs(nrep))
    part_other = lax.ppermute(part, REP, core_pairs(nrep))
    first = jnp.where(core == 0, part, part_other)
    second = jnp.where(core == 0, part_other, part)
    reduced = jnp.stack([first, second], axis=1)
    return (outputs, input_grads, reduced)


def shift_pairs(n, k):
    return [(j, (j + k) % n) for j in range(n)]


def gather_axis(a, axis):
    n = lax.axis_size(axis)
    i = lax.axis_index(axis)
    rows = a.shape[0]
    out = jnp.zeros((n * rows,) + a.shape[1:], a.dtype)
    out = lax.dynamic_update_slice_in_dim(out, a, i * rows, 0)
    for k in range(1, n):
        got = lax.ppermute(a, axis, shift_pairs(n, k))
        out = lax.dynamic_update_slice_in_dim(out, got, ((i - k) % n) * rows, 0)
    return out


def scatter_axis(a, axis, dim=0, wire=None):
    n = lax.axis_size(axis)
    i = lax.axis_index(axis)
    total = lax.dynamic_index_in_dim(a, i, dim, keepdims=False).astype(jnp.float32)
    for k in range(1, n):
        chunk = lax.dynamic_index_in_dim(a, (i + k) % n, dim, keepdims=False)
        if wire is not None:
            chunk = chunk.astype(wire)
        total = total + lax.ppermute(chunk, axis, shift_pairs(n, k)).astype(total.dtype)
    return total


def physical_mesh(mesh):
    devices = np.asarray(mesh.devices)
    flat = devices.reshape(-1)
    nx = len({d.coords[0] for d in flat})
    ny = len({d.coords[1] for d in flat})
    nshard, nrep = mesh.shape["shard"], mesh.shape["rep"]
    shape = (ny, nshard // (nx * ny), nx, nrep // 2, 2)
    return Mesh(devices.reshape(shape), SHARD + REP)


def solution(mesh):
    rows = P(SHARD + REP, None)
    in_specs = (rows, rows, rows, P(SHARD, None, None))
    out_specs = (rows, rows, P(SHARD, None, None))
    return jax.shard_map(
        local, mesh=physical_mesh(mesh), in_specs=in_specs, out_specs=out_specs, check_vma=False
    )
```

```python
import jax
import jax.numpy as jnp
import numpy as np
from jax import lax
from jax.sharding import Mesh
from jax.sharding import PartitionSpec as P

BLOCK = 128


def expert_block(inputs, upstream, expert_slab):
    hidden_width = expert_slab.shape[1] // 3
    gate_up = expert_slab[:, : 2 * hidden_width]
    down_t = expert_slab[:, 2 * hidden_width :]
    project = jnp.dot(inputs, gate_up, preferred_element_type=jnp.float32)
    gate_pre = project[:, :hidden_width]
    up_pre = project[:, hidden_width:]
    gate_sigmoid = jax.nn.sigmoid(gate_pre)
    active = gate_pre * gate_sigmoid
    hidden = (active * up_pre).astype(jnp.bfloat16)
    hidden_grad = jnp.dot(upstream, down_t, preferred_element_type=jnp.float32)
    down_grad = lax.dot_general(
        upstream, hidden, (((0,), (0,)), ((), ())), preferred_element_type=jnp.float32
    )
    gate_grad = hidden_grad * up_pre * gate_sigmoid * (1.0 + gate_pre * (1.0 - gate_sigmoid))
    up_grad = hidden_grad * active
    joint_grad = jnp.concatenate([gate_grad, up_grad], axis=1).astype(jnp.bfloat16)
    proj_grad = lax.dot_general(
        inputs, joint_grad, (((0,), (0,)), ((), ())), preferred_element_type=jnp.float32
    )
    return (hidden, joint_grad, jnp.concatenate([proj_grad, down_grad], axis=1))


def run_expert(expert_slab, inputs, upstream, rows):
    inputs = jnp.where(rows[:, None], inputs, jnp.zeros_like(inputs))
    upstream = jnp.where(rows[:, None], upstream, jnp.zeros_like(upstream))
    return expert_block(inputs, upstream, expert_slab)


SHARD = ("y", "zh", "x")
REP = ("zl", "c")


def core_pairs(n):
    return [(i, i ^ 1) for i in range(n)]


def chip_pairs(n):
    return [(i, i ^ 2) for i in range(n)]


def local(rows_in, cotangent, expert_counts, weights):
    nrep = lax.axis_size(REP)
    core = lax.axis_index("c")
    counts = expert_counts[0]
    padded = (counts + BLOCK - 1) // BLOCK * BLOCK
    starts = jnp.cumsum(padded) - padded
    position = jnp.arange(rows_in.shape[0], dtype=jnp.int32)
    live = (position[:, None] >= starts[None, :]) & (position[:, None] < (starts + counts)[None, :])
    live_mine = jnp.where(core == 0, live[:, 0], live[:, 1])
    live_theirs = jnp.where(core == 0, live[:, 1], live[:, 0])

    mine_local = lax.dynamic_index_in_dim(weights, core, 1, keepdims=False)
    ny, nzh, nx = (lax.axis_size(a) for a in SHARD)
    half = mine_local.shape[0] // 2
    both = gather_axis(mine_local, "zh").reshape(nzh, 2, half, -1)
    first_half = both[:, 0]
    for axis in ("x", "y"):
        first_half = gather_axis(first_half, axis)
    second_half = both[:, 1]
    for axis in ("y", "x"):
        second_half = gather_axis(second_half, axis)
    first_half = first_half.reshape(ny, nx, nzh, half, -1).transpose(0, 2, 1, 3, 4)
    second_half = second_half.reshape(nx, ny, nzh, half, -1).transpose(1, 2, 0, 3, 4)
    mine = jnp.stack([first_half, second_half], axis=3).reshape(-1, mine_local.shape[1])
    theirs = lax.ppermute(mine, REP, core_pairs(nrep))

    hidden_mine, joint_mine, grad_mine = run_expert(mine, rows_in, cotangent, live_mine)
    hidden_theirs, joint_theirs, grad_theirs = run_expert(theirs, rows_in, cotangent, live_theirs)
    width = mine.shape[1] // 3
    contract = (((1,), (1,)), ((), ()))
    outputs = lax.dot_general(
        jnp.concatenate([hidden_mine, hidden_theirs], axis=1),
        jnp.concatenate([mine[:, 2 * width :], theirs[:, 2 * width :]], axis=1),
        contract,
        preferred_element_type=jnp.float32,
    ).astype(jnp.bfloat16)
    input_grads = lax.dot_general(
        jnp.concatenate([joint_mine, joint_theirs], axis=1),
        jnp.concatenate([mine[:, : 2 * width], theirs[:, : 2 * width]], axis=1),
        contract,
        preferred_element_type=jnp.float32,
    ).astype(jnp.bfloat16)
    part = grad_mine + lax.ppermute(grad_theirs, REP, core_pairs(nrep))
    part = part.astype(jnp.bfloat16).reshape(ny, nzh, nx, 2, half, -1)
    first_half = scatter_axis(part[:, :, :, 0], "x", 2)
    second_half = scatter_axis(part[:, :, :, 1], "y", 0)
    first_half = scatter_axis(first_half, "y", 0)
    second_half = scatter_axis(second_half, "x", 1)
    part = scatter_axis(jnp.concatenate([first_half, second_half], axis=1), "zh", 0)
    part = part + lax.ppermute(part, REP, chip_pairs(nrep))
    part_other = lax.ppermute(part, REP, core_pairs(nrep))
    first = jnp.where(core == 0, part, part_other)
    second = jnp.where(core == 0, part_other, part)
    reduced = jnp.stack([first, second], axis=1)
    return (outputs, input_grads, reduced)


def shift_pairs(n, k):
    return [(j, (j + k) % n) for j in range(n)]


def gather_axis(a, axis):
    n = lax.axis_size(axis)
    i = lax.axis_index(axis)
    rows = a.shape[0]
    out = jnp.zeros((n * rows,) + a.shape[1:], a.dtype)
    out = lax.dynamic_update_slice_in_dim(out, a, i * rows, 0)
    for k in range(1, n):
        got = lax.ppermute(a, axis, shift_pairs(n, k))
        out = lax.dynamic_update_slice_in_dim(out, got, ((i - k) % n) * rows, 0)
    return out


def scatter_axis(a, axis, dim=0, wire=None):
    n = lax.axis_size(axis)
    i = lax.axis_index(axis)
    total = lax.dynamic_index_in_dim(a, i, dim, keepdims=False).astype(jnp.float32)
    for k in range(1, n):
        chunk = lax.dynamic_index_in_dim(a, (i + k) % n, dim, keepdims=False)
        if wire is not None:
            chunk = chunk.astype(wire)
        total = total + lax.ppermute(chunk, axis, shift_pairs(n, k)).astype(total.dtype)
    return total


def physical_mesh(mesh):
    devices = np.asarray(mesh.devices)
    flat = devices.reshape(-1)
    nx = len({d.coords[0] for d in flat})
    ny = len({d.coords[1] for d in flat})
    nshard, nrep = mesh.shape["shard"], mesh.shape["rep"]
    shape = (ny, nshard // (nx * ny), nx, nrep // 2, 2)
    return Mesh(devices.reshape(shape), SHARD + REP)


def solution(mesh):
    rows = P(SHARD + REP, None)
    in_specs = (rows, rows, rows, P(SHARD, None, None))
    out_specs = (rows, rows, P(SHARD, None, None))
    return jax.shard_map(
        local, mesh=physical_mesh(mesh), in_specs=in_specs, out_specs=out_specs, check_vma=False
    )
```

```python
import jax
import jax.numpy as jnp
import numpy as np
from jax import lax
from jax.sharding import Mesh
from jax.sharding import PartitionSpec as P

BLOCK = 128


def expert_block(inputs, upstream, expert_slab):
    hidden_width = expert_slab.shape[1] // 3
    gate_up = expert_slab[:, : 2 * hidden_width]
    down_t = expert_slab[:, 2 * hidden_width :]
    project = jnp.dot(inputs, gate_up, preferred_element_type=jnp.float32)
    gate_pre = project[:, :hidden_width]
    up_pre = project[:, hidden_width:]
    gate_sigmoid = jax.nn.sigmoid(gate_pre)
    active = gate_pre * gate_sigmoid
    hidden = (active * up_pre).astype(jnp.bfloat16)
    hidden_grad = jnp.dot(upstream, down_t, preferred_element_type=jnp.float32)
    down_grad = lax.dot_general(
        upstream, hidden, (((0,), (0,)), ((), ())), preferred_element_type=jnp.float32
    )
    gate_grad = hidden_grad * up_pre * gate_sigmoid * (1.0 + gate_pre * (1.0 - gate_sigmoid))
    up_grad = hidden_grad * active
    joint_grad = jnp.concatenate([gate_grad, up_grad], axis=1).astype(jnp.bfloat16)
    proj_grad = lax.dot_general(
        inputs, joint_grad, (((0,), (0,)), ((), ())), preferred_element_type=jnp.float32
    )
    return (hidden, joint_grad, jnp.concatenate([proj_grad, down_grad], axis=1))


def run_expert(expert_slab, inputs, upstream, rows):
    inputs = jnp.where(rows[:, None], inputs, jnp.zeros_like(inputs))
    upstream = jnp.where(rows[:, None], upstream, jnp.zeros_like(upstream))
    return expert_block(inputs, upstream, expert_slab)


SHARD = ("y", "zh", "x")
REP = ("zl", "c")


def core_pairs(n):
    return [(i, i ^ 1) for i in range(n)]


def chip_pairs(n):
    return [(i, i ^ 2) for i in range(n)]


def local(rows_in, cotangent, expert_counts, weights):
    nrep = lax.axis_size(REP)
    core = lax.axis_index("c")
    counts = expert_counts[0]
    padded = (counts + BLOCK - 1) // BLOCK * BLOCK
    starts = jnp.cumsum(padded) - padded
    position = jnp.arange(rows_in.shape[0], dtype=jnp.int32)
    live = (position[:, None] >= starts[None, :]) & (position[:, None] < (starts + counts)[None, :])
    live_mine = jnp.where(core == 0, live[:, 0], live[:, 1])
    live_theirs = jnp.where(core == 0, live[:, 1], live[:, 0])

    mine_local = lax.dynamic_index_in_dim(weights, core, 1, keepdims=False)
    ny, nzh, nx = (lax.axis_size(a) for a in SHARD)
    half = mine_local.shape[0] // 2
    first_half = mine_local[:half]
    for axis in ("zh", "x", "y"):
        first_half = gather_axis(first_half, axis)
    second_half = mine_local[half:]
    for axis in ("zh", "y", "x"):
        second_half = gather_axis(second_half, axis)
    first_half = first_half.reshape(ny, nx, nzh, half, -1).transpose(0, 2, 1, 3, 4)
    second_half = second_half.reshape(nx, ny, nzh, half, -1).transpose(1, 2, 0, 3, 4)
    mine = jnp.stack([first_half, second_half], axis=3).reshape(-1, mine_local.shape[1])
    theirs = lax.ppermute(mine, REP, core_pairs(nrep))

    hidden_mine, joint_mine, grad_mine = run_expert(mine, rows_in, cotangent, live_mine)
    hidden_theirs, joint_theirs, grad_theirs = run_expert(theirs, rows_in, cotangent, live_theirs)
    width = mine.shape[1] // 3
    contract = (((1,), (1,)), ((), ()))
    outputs = lax.dot_general(
        jnp.concatenate([hidden_mine, hidden_theirs], axis=1),
        jnp.concatenate([mine[:, 2 * width :], theirs[:, 2 * width :]], axis=1),
        contract,
        preferred_element_type=jnp.float32,
    ).astype(jnp.bfloat16)
    input_grads = lax.dot_general(
        jnp.concatenate([joint_mine, joint_theirs], axis=1),
        jnp.concatenate([mine[:, : 2 * width], theirs[:, : 2 * width]], axis=1),
        contract,
        preferred_element_type=jnp.float32,
    ).astype(jnp.bfloat16)
    part = grad_mine + lax.ppermute(grad_theirs, REP, core_pairs(nrep))
    part = part.astype(jnp.bfloat16).reshape(ny, nzh, nx, 2, half, -1)
    first_half = scatter_axis(part[:, :, :, 0], "x", 2)
    second_half = scatter_axis(part[:, :, :, 1], "y", 0)
    first_half = scatter_axis(scatter_axis(first_half, "y", 0), "zh", 0)
    second_half = scatter_axis(scatter_axis(second_half, "x", 1), "zh", 0)
    part = jnp.concatenate([first_half, second_half], axis=0)
    part = part + lax.ppermute(part, REP, chip_pairs(nrep))
    part_other = lax.ppermute(part, REP, core_pairs(nrep))
    first = jnp.where(core == 0, part, part_other)
    second = jnp.where(core == 0, part_other, part)
    reduced = jnp.stack([first, second], axis=1)
    return (outputs, input_grads, reduced)


def shift_pairs(n, k):
    return [(j, (j + k) % n) for j in range(n)]


def gather_axis(a, axis):
    n = lax.axis_size(axis)
    i = lax.axis_index(axis)
    rows = a.shape[0]
    out = jnp.zeros((n * rows,) + a.shape[1:], a.dtype)
    out = lax.dynamic_update_slice_in_dim(out, a, i * rows, 0)
    for k in range(1, n):
        got = lax.ppermute(a, axis, shift_pairs(n, k))
        out = lax.dynamic_update_slice_in_dim(out, got, ((i - k) % n) * rows, 0)
    return out


def scatter_axis(a, axis, dim=0, wire=None):
    n = lax.axis_size(axis)
    i = lax.axis_index(axis)
    total = lax.dynamic_index_in_dim(a, i, dim, keepdims=False).astype(jnp.float32)
    for k in range(1, n):
        chunk = lax.dynamic_index_in_dim(a, (i + k) % n, dim, keepdims=False)
        if wire is not None:
            chunk = chunk.astype(wire)
        total = total + lax.ppermute(chunk, axis, shift_pairs(n, k)).astype(total.dtype)
    return total


def physical_mesh(mesh):
    devices = np.asarray(mesh.devices)
    flat = devices.reshape(-1)
    nx = len({d.coords[0] for d in flat})
    ny = len({d.coords[1] for d in flat})
    nshard, nrep = mesh.shape["shard"], mesh.shape["rep"]
    shape = (ny, nshard // (nx * ny), nx, nrep // 2, 2)
    return Mesh(devices.reshape(shape), SHARD + REP)


def solution(mesh):
    rows = P(SHARD + REP, None)
    in_specs = (rows, rows, rows, P(SHARD, None, None))
    out_specs = (rows, rows, P(SHARD, None, None))
    return jax.shard_map(
        local, mesh=physical_mesh(mesh), in_specs=in_specs, out_specs=out_specs, check_vma=False
    )
```

```python
import jax
import jax.numpy as jnp
import numpy as np
from jax import lax
from jax.sharding import Mesh
from jax.sharding import PartitionSpec as P

BLOCK = 128


def expert_block(inputs, upstream, expert_slab):
    hidden_width = expert_slab.shape[1] // 3
    gate_up = expert_slab[:, : 2 * hidden_width]
    down_t = expert_slab[:, 2 * hidden_width :]
    project = jnp.dot(inputs, gate_up, preferred_element_type=jnp.float32)
    gate_pre = project[:, :hidden_width]
    up_pre = project[:, hidden_width:]
    gate_sigmoid = jax.nn.sigmoid(gate_pre)
    active = gate_pre * gate_sigmoid
    hidden = (active * up_pre).astype(jnp.bfloat16)
    output = lax.dot_general(
        hidden, down_t, (((1,), (1,)), ((), ())), preferred_element_type=jnp.float32
    ).astype(jnp.bfloat16)
    hidden_grad = jnp.dot(upstream, down_t, preferred_element_type=jnp.float32)
    down_grad = lax.dot_general(
        upstream, hidden, (((0,), (0,)), ((), ())), preferred_element_type=jnp.float32
    )
    gate_grad = hidden_grad * up_pre * gate_sigmoid * (1.0 + gate_pre * (1.0 - gate_sigmoid))
    up_grad = hidden_grad * active
    joint_grad = jnp.concatenate([gate_grad, up_grad], axis=1).astype(jnp.bfloat16)
    proj_grad = lax.dot_general(
        inputs, joint_grad, (((0,), (0,)), ((), ())), preferred_element_type=jnp.float32
    )
    input_grad = lax.dot_general(
        joint_grad, gate_up, (((1,), (1,)), ((), ())), preferred_element_type=jnp.float32
    ).astype(jnp.bfloat16)
    return (output, input_grad, jnp.concatenate([proj_grad, down_grad], axis=1))


def run_expert(expert_slab, inputs, upstream, rows):
    inputs = jnp.where(rows[:, None], inputs, jnp.zeros_like(inputs))
    upstream = jnp.where(rows[:, None], upstream, jnp.zeros_like(upstream))
    return expert_block(inputs, upstream, expert_slab)


SHARD = ("y", "zh", "x")
REP = ("zl", "c")


def core_pairs(n):
    return [(i, i ^ 1) for i in range(n)]


def chip_pairs(n):
    return [(i, i ^ 2) for i in range(n)]


def local(rows_in, cotangent, expert_counts, weights):
    nrep = lax.axis_size(REP)
    core = lax.axis_index("c")
    counts = expert_counts[0]
    padded = (counts + BLOCK - 1) // BLOCK * BLOCK
    starts = jnp.cumsum(padded) - padded
    position = jnp.arange(rows_in.shape[0], dtype=jnp.int32)
    live = (position[:, None] >= starts[None, :]) & (position[:, None] < (starts + counts)[None, :])
    live_mine = jnp.where(core == 0, live[:, 0], live[:, 1])
    live_theirs = jnp.where(core == 0, live[:, 1], live[:, 0])

    mine_local = lax.dynamic_index_in_dim(weights, core, 1, keepdims=False)
    ny, nzh, nx = (lax.axis_size(a) for a in SHARD)
    half = mine_local.shape[0] // 2
    first_half = mine_local[:half]
    for axis in ("zh", "x", "y"):
        first_half = gather_axis(first_half, axis)
    second_half = mine_local[half:]
    for axis in ("zh", "y", "x"):
        second_half = gather_axis(second_half, axis)
    first_half = first_half.reshape(ny, nx, nzh, half, -1).transpose(0, 2, 1, 3, 4)
    second_half = second_half.reshape(nx, ny, nzh, half, -1).transpose(1, 2, 0, 3, 4)
    mine = jnp.stack([first_half, second_half], axis=3).reshape(-1, mine_local.shape[1])
    theirs = lax.ppermute(mine, REP, core_pairs(nrep))

    out_mine, in_grad_mine, grad_mine = run_expert(mine, rows_in, cotangent, live_mine)
    out_theirs, in_grad_theirs, grad_theirs = run_expert(theirs, rows_in, cotangent, live_theirs)
    zero = jnp.zeros_like(rows_in)
    outputs = jnp.where(
        live_mine[:, None], out_mine, jnp.where(live_theirs[:, None], out_theirs, zero)
    )
    input_grads = jnp.where(
        live_mine[:, None], in_grad_mine, jnp.where(live_theirs[:, None], in_grad_theirs, zero)
    )
    part = grad_mine + lax.ppermute(grad_theirs, REP, core_pairs(nrep))
    part = part.astype(jnp.bfloat16).reshape(ny, nzh, nx, 2, half, -1)
    first_half = scatter_axis(part[:, :, :, 0], "x", 2)
    second_half = scatter_axis(part[:, :, :, 1], "y", 0)
    first_half = scatter_axis(scatter_axis(first_half, "y", 0, jnp.bfloat16), "zh", 0)
    second_half = scatter_axis(scatter_axis(second_half, "x", 1, jnp.bfloat16), "zh", 0)
    part = jnp.concatenate([first_half, second_half], axis=0)
    part = part + lax.ppermute(part, REP, chip_pairs(nrep))
    part_other = lax.ppermute(part, REP, core_pairs(nrep))
    first = jnp.where(core == 0, part, part_other)
    second = jnp.where(core == 0, part_other, part)
    reduced = jnp.stack([first, second], axis=1)
    return (outputs, input_grads, reduced)


def shift_pairs(n, k):
    return [(j, (j + k) % n) for j in range(n)]


def gather_axis(a, axis):
    n = lax.axis_size(axis)
    i = lax.axis_index(axis)
    rows = a.shape[0]
    out = jnp.zeros((n * rows,) + a.shape[1:], a.dtype)
    out = lax.dynamic_update_slice_in_dim(out, a, i * rows, 0)
    for k in range(1, n):
        got = lax.ppermute(a, axis, shift_pairs(n, k))
        out = lax.dynamic_update_slice_in_dim(out, got, ((i - k) % n) * rows, 0)
    return out


def scatter_axis(a, axis, dim=0, wire=None):
    n = lax.axis_size(axis)
    i = lax.axis_index(axis)
    total = lax.dynamic_index_in_dim(a, i, dim, keepdims=False).astype(jnp.float32)
    for k in range(1, n):
        chunk = lax.dynamic_index_in_dim(a, (i + k) % n, dim, keepdims=False)
        if wire is not None:
            chunk = chunk.astype(wire)
        total = total + lax.ppermute(chunk, axis, shift_pairs(n, k)).astype(total.dtype)
    return total


def physical_mesh(mesh):
    devices = np.asarray(mesh.devices)
    flat = devices.reshape(-1)
    nx = len({d.coords[0] for d in flat})
    ny = len({d.coords[1] for d in flat})
    nshard, nrep = mesh.shape["shard"], mesh.shape["rep"]
    shape = (ny, nshard // (nx * ny), nx, nrep // 2, 2)
    return Mesh(devices.reshape(shape), SHARD + REP)


def solution(mesh):
    rows = P(SHARD + REP, None)
    in_specs = (rows, rows, rows, P(SHARD, None, None))
    out_specs = (rows, rows, P(SHARD, None, None))
    return jax.shard_map(
        local, mesh=physical_mesh(mesh), in_specs=in_specs, out_specs=out_specs, check_vma=False
    )
```

```python
import jax
import jax.numpy as jnp
import numpy as np
from jax import lax
from jax.sharding import Mesh
from jax.sharding import PartitionSpec as P

BLOCK = 128


def expert_block(inputs, upstream, expert_slab):
    hidden_width = expert_slab.shape[1] // 3
    gate_up = expert_slab[:, : 2 * hidden_width]
    down_t = expert_slab[:, 2 * hidden_width :]
    project = jnp.dot(inputs, gate_up, preferred_element_type=jnp.float32)
    gate_pre = project[:, :hidden_width]
    up_pre = project[:, hidden_width:]
    gate_sigmoid = jax.nn.sigmoid(gate_pre)
    active = gate_pre * gate_sigmoid
    hidden = (active * up_pre).astype(jnp.bfloat16)
    output = lax.dot_general(
        hidden, down_t, (((1,), (1,)), ((), ())), preferred_element_type=jnp.float32
    ).astype(jnp.bfloat16)
    hidden_grad = jnp.dot(upstream, down_t, preferred_element_type=jnp.float32)
    down_grad = lax.dot_general(
        upstream, hidden, (((0,), (0,)), ((), ())), preferred_element_type=jnp.float32
    )
    gate_grad = hidden_grad * up_pre * gate_sigmoid * (1.0 + gate_pre * (1.0 - gate_sigmoid))
    up_grad = hidden_grad * active
    joint_grad = jnp.concatenate([gate_grad, up_grad], axis=1).astype(jnp.bfloat16)
    proj_grad = lax.dot_general(
        inputs, joint_grad, (((0,), (0,)), ((), ())), preferred_element_type=jnp.float32
    )
    input_grad = lax.dot_general(
        joint_grad, gate_up, (((1,), (1,)), ((), ())), preferred_element_type=jnp.float32
    ).astype(jnp.bfloat16)
    return (output, input_grad, jnp.concatenate([proj_grad, down_grad], axis=1))


def run_expert(expert_slab, inputs, upstream, rows):
    inputs = jnp.where(rows[:, None], inputs, jnp.zeros_like(inputs))
    upstream = jnp.where(rows[:, None], upstream, jnp.zeros_like(upstream))
    return expert_block(inputs, upstream, expert_slab)


SHARD = ("y", "zh", "x")
REP = ("zl", "c")


def core_pairs(n):
    return [(i, i ^ 1) for i in range(n)]


def chip_pairs(n):
    return [(i, i ^ 2) for i in range(n)]


def local(rows_in, cotangent, expert_counts, weights):
    nrep = lax.axis_size(REP)
    core = lax.axis_index("c")
    counts = expert_counts[0]
    padded = (counts + BLOCK - 1) // BLOCK * BLOCK
    starts = jnp.cumsum(padded) - padded
    position = jnp.arange(rows_in.shape[0], dtype=jnp.int32)
    live = (position[:, None] >= starts[None, :]) & (position[:, None] < (starts + counts)[None, :])
    live_mine = jnp.where(core == 0, live[:, 0], live[:, 1])
    live_theirs = jnp.where(core == 0, live[:, 1], live[:, 0])

    mine_local = lax.dynamic_index_in_dim(weights, core, 1, keepdims=False)
    ny, nzh, nx = (lax.axis_size(a) for a in SHARD)
    half = mine_local.shape[0] // 2
    first_half = mine_local[:half]
    for axis in ("zh", "x", "y"):
        first_half = gather_axis(first_half, axis)
    second_half = mine_local[half:]
    for axis in ("zh", "y", "x"):
        second_half = gather_axis(second_half, axis)
    first_half = first_half.reshape(ny, nx, nzh, half, -1).transpose(0, 2, 1, 3, 4)
    second_half = second_half.reshape(nx, ny, nzh, half, -1).transpose(1, 2, 0, 3, 4)
    mine = jnp.stack([first_half, second_half], axis=3).reshape(-1, mine_local.shape[1])
    theirs = lax.ppermute(mine, REP, core_pairs(nrep))

    out_mine, in_grad_mine, grad_mine = run_expert(mine, rows_in, cotangent, live_mine)
    out_theirs, in_grad_theirs, grad_theirs = run_expert(theirs, rows_in, cotangent, live_theirs)
    zero = jnp.zeros_like(rows_in)
    outputs = jnp.where(
        live_mine[:, None], out_mine, jnp.where(live_theirs[:, None], out_theirs, zero)
    )
    input_grads = jnp.where(
        live_mine[:, None], in_grad_mine, jnp.where(live_theirs[:, None], in_grad_theirs, zero)
    )
    part = grad_mine + lax.ppermute(
        grad_theirs.astype(jnp.bfloat16), REP, core_pairs(nrep)
    ).astype(jnp.float32)
    part = part.astype(jnp.bfloat16).reshape(ny, nzh, nx, 2, half, -1)
    first_half = scatter_axis(part[:, :, :, 0], "x", 2)
    second_half = scatter_axis(part[:, :, :, 1], "y", 0)
    first_half = scatter_axis(scatter_axis(first_half, "y", 0, jnp.bfloat16), "zh", 0, jnp.bfloat16)
    second_half = scatter_axis(scatter_axis(second_half, "x", 1, jnp.bfloat16), "zh", 0, jnp.bfloat16)
    part = jnp.concatenate([first_half, second_half], axis=0)
    part = part + lax.ppermute(part, REP, chip_pairs(nrep))
    part_other = lax.ppermute(part, REP, core_pairs(nrep))
    first = jnp.where(core == 0, part, part_other)
    second = jnp.where(core == 0, part_other, part)
    reduced = jnp.stack([first, second], axis=1)
    return (outputs, input_grads, reduced)


def shift_pairs(n, k):
    return [(j, (j + k) % n) for j in range(n)]


def gather_axis(a, axis):
    n = lax.axis_size(axis)
    i = lax.axis_index(axis)
    rows = a.shape[0]
    out = jnp.zeros((n * rows,) + a.shape[1:], a.dtype)
    out = lax.dynamic_update_slice_in_dim(out, a, i * rows, 0)
    for k in range(1, n):
        got = lax.ppermute(a, axis, shift_pairs(n, k))
        out = lax.dynamic_update_slice_in_dim(out, got, ((i - k) % n) * rows, 0)
    return out


def scatter_axis(a, axis, dim=0, wire=None):
    n = lax.axis_size(axis)
    i = lax.axis_index(axis)
    total = lax.dynamic_index_in_dim(a, i, dim, keepdims=False).astype(jnp.float32)
    for k in range(1, n):
        chunk = lax.dynamic_index_in_dim(a, (i + k) % n, dim, keepdims=False)
        if wire is not None:
            chunk = chunk.astype(wire)
        total = total + lax.ppermute(chunk, axis, shift_pairs(n, k)).astype(total.dtype)
    return total


def physical_mesh(mesh):
    devices = np.asarray(mesh.devices)
    flat = devices.reshape(-1)
    nx = len({d.coords[0] for d in flat})
    ny = len({d.coords[1] for d in flat})
    nshard, nrep = mesh.shape["shard"], mesh.shape["rep"]
    shape = (ny, nshard // (nx * ny), nx, nrep // 2, 2)
    return Mesh(devices.reshape(shape), SHARD + REP)


def solution(mesh):
    rows = P(SHARD + REP, None)
    in_specs = (rows, rows, rows, P(SHARD, None, None))
    out_specs = (rows, rows, P(SHARD, None, None))
    return jax.shard_map(
        local, mesh=physical_mesh(mesh), in_specs=in_specs, out_specs=out_specs, check_vma=False
    )
```

```python
import jax
import jax.numpy as jnp
import numpy as np
from jax import lax
from jax.sharding import Mesh
from jax.sharding import PartitionSpec as P

BLOCK = 128


def expert_block(inputs, upstream, expert_slab):
    hidden_width = expert_slab.shape[1] // 3
    gate_up = expert_slab[:, : 2 * hidden_width]
    down_t = expert_slab[:, 2 * hidden_width :]
    project = jnp.dot(inputs, gate_up, preferred_element_type=jnp.float32)
    gate_pre = project[:, :hidden_width]
    up_pre = project[:, hidden_width:]
    gate_sigmoid = jax.nn.sigmoid(gate_pre)
    active = gate_pre * gate_sigmoid
    hidden = (active * up_pre).astype(jnp.bfloat16)
    output = lax.dot_general(
        hidden, down_t, (((1,), (1,)), ((), ())), preferred_element_type=jnp.float32
    ).astype(jnp.bfloat16)
    hidden_grad = jnp.dot(upstream, down_t, preferred_element_type=jnp.float32)
    down_grad = lax.dot_general(
        upstream, hidden, (((0,), (0,)), ((), ())), preferred_element_type=jnp.float32
    )
    gate_grad = hidden_grad * up_pre * gate_sigmoid * (1.0 + gate_pre * (1.0 - gate_sigmoid))
    up_grad = hidden_grad * active
    joint_grad = jnp.concatenate([gate_grad, up_grad], axis=1).astype(jnp.bfloat16)
    proj_grad = lax.dot_general(
        inputs, joint_grad, (((0,), (0,)), ((), ())), preferred_element_type=jnp.float32
    )
    input_grad = lax.dot_general(
        joint_grad, gate_up, (((1,), (1,)), ((), ())), preferred_element_type=jnp.float32
    ).astype(jnp.bfloat16)
    return (output, input_grad, jnp.concatenate([proj_grad, down_grad], axis=1))


def run_expert(expert_slab, inputs, upstream, rows):
    inputs = jnp.where(rows[:, None], inputs, jnp.zeros_like(inputs))
    upstream = jnp.where(rows[:, None], upstream, jnp.zeros_like(upstream))
    return expert_block(inputs, upstream, expert_slab)


SHARD = ("y", "zh", "x")
REP = ("zl", "c")


def core_pairs(n):
    return [(i, i ^ 1) for i in range(n)]


def chip_pairs(n):
    return [(i, i ^ 2) for i in range(n)]


def local(rows_in, cotangent, expert_counts, weights):
    nrep = lax.axis_size(REP)
    core = lax.axis_index("c")
    counts = expert_counts[0]
    padded = (counts + BLOCK - 1) // BLOCK * BLOCK
    starts = jnp.cumsum(padded) - padded
    position = jnp.arange(rows_in.shape[0], dtype=jnp.int32)
    live = (position[:, None] >= starts[None, :]) & (position[:, None] < (starts + counts)[None, :])
    live_mine = jnp.where(core == 0, live[:, 0], live[:, 1])
    live_theirs = jnp.where(core == 0, live[:, 1], live[:, 0])

    mine_local = lax.dynamic_index_in_dim(weights, core, 1, keepdims=False)
    ny, nzh, nx = (lax.axis_size(a) for a in SHARD)
    half = mine_local.shape[0] // 2
    first_half = mine_local[:half]
    for axis in ("zh", "x", "y"):
        first_half = gather_axis(first_half, axis)
    second_half = mine_local[half:]
    for axis in ("zh", "y", "x"):
        second_half = gather_axis(second_half, axis)
    first_half = first_half.reshape(ny, nx, nzh, half, -1).transpose(0, 2, 1, 3, 4)
    second_half = second_half.reshape(nx, ny, nzh, half, -1).transpose(1, 2, 0, 3, 4)
    mine = jnp.stack([first_half, second_half], axis=3).reshape(-1, mine_local.shape[1])
    theirs = lax.ppermute(mine, REP, core_pairs(nrep))

    out_mine, in_grad_mine, grad_mine = run_expert(mine, rows_in, cotangent, live_mine)
    theirs, out_mine, in_grad_mine, grad_mine = lax.optimization_barrier(
        (theirs, out_mine, in_grad_mine, grad_mine)
    )
    out_theirs, in_grad_theirs, grad_theirs = run_expert(theirs, rows_in, cotangent, live_theirs)
    zero = jnp.zeros_like(rows_in)
    outputs = jnp.where(
        live_mine[:, None], out_mine, jnp.where(live_theirs[:, None], out_theirs, zero)
    )
    input_grads = jnp.where(
        live_mine[:, None], in_grad_mine, jnp.where(live_theirs[:, None], in_grad_theirs, zero)
    )
    part = grad_mine + lax.ppermute(grad_theirs, REP, core_pairs(nrep))
    part = part.astype(jnp.bfloat16).reshape(ny, nzh, nx, 2, half, -1)
    first_half = scatter_axis(part[:, :, :, 0], "x", 2)
    second_half = scatter_axis(part[:, :, :, 1], "y", 0)
    first_half = scatter_axis(scatter_axis(first_half, "y", 0, jnp.bfloat16), "zh", 0)
    second_half = scatter_axis(scatter_axis(second_half, "x", 1, jnp.bfloat16), "zh", 0)
    part = jnp.concatenate([first_half, second_half], axis=0)
    part = part + lax.ppermute(part, REP, chip_pairs(nrep))
    part_other = lax.ppermute(part, REP, core_pairs(nrep))
    first = jnp.where(core == 0, part, part_other)
    second = jnp.where(core == 0, part_other, part)
    reduced = jnp.stack([first, second], axis=1)
    return (outputs, input_grads, reduced)


def shift_pairs(n, k):
    return [(j, (j + k) % n) for j in range(n)]


def gather_axis(a, axis):
    n = lax.axis_size(axis)
    i = lax.axis_index(axis)
    rows = a.shape[0]
    out = jnp.zeros((n * rows,) + a.shape[1:], a.dtype)
    out = lax.dynamic_update_slice_in_dim(out, a, i * rows, 0)
    for k in range(1, n):
        got = lax.ppermute(a, axis, shift_pairs(n, k))
        out = lax.dynamic_update_slice_in_dim(out, got, ((i - k) % n) * rows, 0)
    return out


def scatter_axis(a, axis, dim=0, wire=None):
    n = lax.axis_size(axis)
    i = lax.axis_index(axis)
    total = lax.dynamic_index_in_dim(a, i, dim, keepdims=False).astype(jnp.float32)
    for k in range(1, n):
        chunk = lax.dynamic_index_in_dim(a, (i + k) % n, dim, keepdims=False)
        if wire is not None:
            chunk = chunk.astype(wire)
        total = total + lax.ppermute(chunk, axis, shift_pairs(n, k)).astype(total.dtype)
    return total


def physical_mesh(mesh):
    devices = np.asarray(mesh.devices)
    flat = devices.reshape(-1)
    nx = len({d.coords[0] for d in flat})
    ny = len({d.coords[1] for d in flat})
    nshard, nrep = mesh.shape["shard"], mesh.shape["rep"]
    shape = (ny, nshard // (nx * ny), nx, nrep // 2, 2)
    return Mesh(devices.reshape(shape), SHARD + REP)


def solution(mesh):
    rows = P(SHARD + REP, None)
    in_specs = (rows, rows, rows, P(SHARD, None, None))
    out_specs = (rows, rows, P(SHARD, None, None))
    return jax.shard_map(
        local, mesh=physical_mesh(mesh), in_specs=in_specs, out_specs=out_specs, check_vma=False
    )
```

```python
import jax
import jax.numpy as jnp
import numpy as np
from jax import lax
from jax.sharding import Mesh
from jax.sharding import PartitionSpec as P

BLOCK = 128


def expert_block(inputs, upstream, expert_slab):
    hidden_width = expert_slab.shape[1] // 3
    gate_up = expert_slab[:, : 2 * hidden_width]
    down_t = expert_slab[:, 2 * hidden_width :]
    project = jnp.dot(inputs, gate_up, preferred_element_type=jnp.float32)
    gate_pre = project[:, :hidden_width]
    up_pre = project[:, hidden_width:]
    gate_sigmoid = jax.nn.sigmoid(gate_pre)
    active = gate_pre * gate_sigmoid
    hidden = (active * up_pre).astype(jnp.bfloat16)
    output = lax.dot_general(
        hidden, down_t, (((1,), (1,)), ((), ())), preferred_element_type=jnp.float32
    ).astype(jnp.bfloat16)
    hidden_grad = jnp.dot(upstream, down_t, preferred_element_type=jnp.float32)
    down_grad = lax.dot_general(
        upstream, hidden, (((0,), (0,)), ((), ())), preferred_element_type=jnp.float32
    )
    gate_grad = hidden_grad * up_pre * gate_sigmoid * (1.0 + gate_pre * (1.0 - gate_sigmoid))
    up_grad = hidden_grad * active
    joint_grad = jnp.concatenate([gate_grad, up_grad], axis=1).astype(jnp.bfloat16)
    proj_grad = lax.dot_general(
        inputs, joint_grad, (((0,), (0,)), ((), ())), preferred_element_type=jnp.float32
    )
    input_grad = lax.dot_general(
        joint_grad, gate_up, (((1,), (1,)), ((), ())), preferred_element_type=jnp.float32
    ).astype(jnp.bfloat16)
    return (output, input_grad, jnp.concatenate([proj_grad, down_grad], axis=1))


def run_expert(expert_slab, inputs, upstream, rows):
    inputs = jnp.where(rows[:, None], inputs, jnp.zeros_like(inputs))
    upstream = jnp.where(rows[:, None], upstream, jnp.zeros_like(upstream))
    return expert_block(inputs, upstream, expert_slab)


SHARD = ("y", "zh", "x")
REP = ("zl", "c")


def core_pairs(n):
    return [(i, i ^ 1) for i in range(n)]


def chip_pairs(n):
    return [(i, i ^ 2) for i in range(n)]


def local(rows_in, cotangent, expert_counts, weights):
    nrep = lax.axis_size(REP)
    core = lax.axis_index("c")
    counts = expert_counts[0]
    padded = (counts + BLOCK - 1) // BLOCK * BLOCK
    starts = jnp.cumsum(padded) - padded
    position = jnp.arange(rows_in.shape[0], dtype=jnp.int32)
    live = (position[:, None] >= starts[None, :]) & (position[:, None] < (starts + counts)[None, :])
    live_mine = jnp.where(core == 0, live[:, 0], live[:, 1])
    live_theirs = jnp.where(core == 0, live[:, 1], live[:, 0])

    mine_local = lax.dynamic_index_in_dim(weights, core, 1, keepdims=False)
    ny, nzh, nx = (lax.axis_size(a) for a in SHARD)
    half = mine_local.shape[0] // 2
    first_half = mine_local[:half]
    for axis in ("zh", "x", "y"):
        first_half = gather_axis(first_half, axis)
    second_half = mine_local[half:]
    for axis in ("zh", "y", "x"):
        second_half = gather_axis(second_half, axis)
    first_half = first_half.reshape(ny, nx, nzh, half, -1).transpose(0, 2, 1, 3, 4)
    second_half = second_half.reshape(nx, ny, nzh, half, -1).transpose(1, 2, 0, 3, 4)
    mine = jnp.stack([first_half, second_half], axis=3).reshape(-1, mine_local.shape[1])
    theirs = lax.ppermute(mine, REP, core_pairs(nrep))

    out_mine, in_grad_mine, grad_mine = run_expert(mine, rows_in, cotangent, live_mine)
    out_theirs, in_grad_theirs, grad_theirs = run_expert(theirs, rows_in, cotangent, live_theirs)
    zero = jnp.zeros_like(rows_in)
    outputs = jnp.where(
        live_mine[:, None], out_mine, jnp.where(live_theirs[:, None], out_theirs, zero)
    )
    input_grads = jnp.where(
        live_mine[:, None], in_grad_mine, jnp.where(live_theirs[:, None], in_grad_theirs, zero)
    )
    part = grad_mine + lax.ppermute(grad_theirs, REP, core_pairs(nrep))
    part = part.astype(jnp.bfloat16).reshape(ny, nzh, nx, 2, half, -1)
    first_half = scatter_axis(part[:, :, :, 0], "x", 2)
    second_half = scatter_axis(part[:, :, :, 1], "y", 0)
    first_half = scatter_axis(scatter_axis(first_half, "y", 0, jnp.bfloat16), "zh", 0, jnp.bfloat16)
    second_half = scatter_axis(scatter_axis(second_half, "x", 1, jnp.bfloat16), "zh", 0, jnp.bfloat16)
    part = jnp.concatenate([first_half, second_half], axis=0)
    part = part + lax.ppermute(part, REP, chip_pairs(nrep))
    part_other = lax.ppermute(part, REP, core_pairs(nrep))
    first = jnp.where(core == 0, part, part_other)
    second = jnp.where(core == 0, part_other, part)
    reduced = jnp.stack([first, second], axis=1)
    return (outputs, input_grads, reduced)


def shift_pairs(n, k):
    return [(j, (j + k) % n) for j in range(n)]


def gather_axis(a, axis):
    n = lax.axis_size(axis)
    i = lax.axis_index(axis)
    rows = a.shape[0]
    out = jnp.zeros((n * rows,) + a.shape[1:], a.dtype)
    out = lax.dynamic_update_slice_in_dim(out, a, i * rows, 0)
    for k in range(1, n):
        got = lax.ppermute(a, axis, shift_pairs(n, k))
        out = lax.dynamic_update_slice_in_dim(out, got, ((i - k) % n) * rows, 0)
    return out


def scatter_axis(a, axis, dim=0, wire=None):
    n = lax.axis_size(axis)
    i = lax.axis_index(axis)
    total = lax.dynamic_index_in_dim(a, i, dim, keepdims=False).astype(jnp.float32)
    for k in range(1, n):
        chunk = lax.dynamic_index_in_dim(a, (i + k) % n, dim, keepdims=False)
        if wire is not None:
            chunk = chunk.astype(wire)
        total = total + lax.ppermute(chunk, axis, shift_pairs(n, k)).astype(total.dtype)
    return total


def physical_mesh(mesh):
    devices = np.asarray(mesh.devices)
    flat = devices.reshape(-1)
    nx = len({d.coords[0] for d in flat})
    ny = len({d.coords[1] for d in flat})
    nshard, nrep = mesh.shape["shard"], mesh.shape["rep"]
    shape = (ny, nshard // (nx * ny), nx, nrep // 2, 2)
    return Mesh(devices.reshape(shape), SHARD + REP)


def solution(mesh):
    rows = P(SHARD + REP, None)
    in_specs = (rows, rows, rows, P(SHARD, None, None))
    out_specs = (rows, rows, P(SHARD, None, None))
    return jax.shard_map(
        local, mesh=physical_mesh(mesh), in_specs=in_specs, out_specs=out_specs, check_vma=False
    )
```

```python
import jax
import jax.numpy as jnp
import numpy as np
from jax import lax
from jax.sharding import Mesh
from jax.sharding import PartitionSpec as P

BLOCK = 128


def expert_block(inputs, upstream, expert_slab):
    hidden_width = expert_slab.shape[1] // 3
    gate_up = expert_slab[:, : 2 * hidden_width]
    down_t = expert_slab[:, 2 * hidden_width :]
    project = jnp.dot(inputs, gate_up, preferred_element_type=jnp.float32)
    gate_pre = project[:, :hidden_width]
    up_pre = project[:, hidden_width:]
    gate_sigmoid = jax.nn.sigmoid(gate_pre)
    active = gate_pre * gate_sigmoid
    hidden = (active * up_pre).astype(jnp.bfloat16)
    output = lax.dot_general(
        hidden, down_t, (((1,), (1,)), ((), ())), preferred_element_type=jnp.float32
    ).astype(jnp.bfloat16)
    hidden_grad = jnp.dot(upstream, down_t, preferred_element_type=jnp.float32)
    down_grad = lax.dot_general(
        upstream, hidden, (((0,), (0,)), ((), ())), preferred_element_type=jnp.float32
    )
    gate_grad = hidden_grad * up_pre * gate_sigmoid * (1.0 + gate_pre * (1.0 - gate_sigmoid))
    up_grad = hidden_grad * active
    joint_grad = jnp.concatenate([gate_grad, up_grad], axis=1).astype(jnp.bfloat16)
    proj_grad = lax.dot_general(
        inputs, joint_grad, (((0,), (0,)), ((), ())), preferred_element_type=jnp.float32
    )
    input_grad = lax.dot_general(
        joint_grad, gate_up, (((1,), (1,)), ((), ())), preferred_element_type=jnp.float32
    ).astype(jnp.bfloat16)
    return (output, input_grad, jnp.concatenate([proj_grad, down_grad], axis=1))


def run_expert(expert_slab, inputs, upstream, rows):
    inputs = jnp.where(rows[:, None], inputs, jnp.zeros_like(inputs))
    upstream = jnp.where(rows[:, None], upstream, jnp.zeros_like(upstream))
    return expert_block(inputs, upstream, expert_slab)


SHARD = ("y", "zh", "x")
REP = ("zl", "c")


def core_pairs(n):
    return [(i, i ^ 1) for i in range(n)]


def chip_pairs(n):
    return [(i, i ^ 2) for i in range(n)]


def local(rows_in, cotangent, expert_counts, weights):
    nrep = lax.axis_size(REP)
    core = lax.axis_index("c")
    counts = expert_counts[0]
    padded = (counts + BLOCK - 1) // BLOCK * BLOCK
    starts = jnp.cumsum(padded) - padded
    position = jnp.arange(rows_in.shape[0], dtype=jnp.int32)
    live = (position[:, None] >= starts[None, :]) & (position[:, None] < (starts + counts)[None, :])
    live_mine = jnp.where(core == 0, live[:, 0], live[:, 1])
    live_theirs = jnp.where(core == 0, live[:, 1], live[:, 0])

    mine_local = lax.dynamic_index_in_dim(weights, core, 1, keepdims=False)
    ny, nzh, nx = (lax.axis_size(a) for a in SHARD)
    half = mine_local.shape[0] // 2
    both = gather_axis(mine_local, "zh").reshape(nzh, 2, half, -1)
    first_half = both[:, 0]
    for axis in ("x", "y"):
        first_half = gather_axis(first_half, axis)
    second_half = both[:, 1]
    for axis in ("y", "x"):
        second_half = gather_axis(second_half, axis)
    first_half = first_half.reshape(ny, nx, nzh, half, -1).transpose(0, 2, 1, 3, 4)
    second_half = second_half.reshape(nx, ny, nzh, half, -1).transpose(1, 2, 0, 3, 4)
    mine = jnp.stack([first_half, second_half], axis=3).reshape(-1, mine_local.shape[1])
    theirs = lax.ppermute(mine, REP, core_pairs(nrep))

    out_mine, in_grad_mine, grad_mine = run_expert(mine, rows_in, cotangent, live_mine)
    out_theirs, in_grad_theirs, grad_theirs = run_expert(theirs, rows_in, cotangent, live_theirs)
    zero = jnp.zeros_like(rows_in)
    outputs = jnp.where(
        live_mine[:, None], out_mine, jnp.where(live_theirs[:, None], out_theirs, zero)
    )
    input_grads = jnp.where(
        live_mine[:, None], in_grad_mine, jnp.where(live_theirs[:, None], in_grad_theirs, zero)
    )
    part = grad_mine + lax.ppermute(grad_theirs, REP, core_pairs(nrep))
    part = part.astype(jnp.bfloat16).reshape(ny, nzh, nx, 2, half, -1)
    first_half = scatter_axis(part[:, :, :, 0], "x", 2)
    second_half = scatter_axis(part[:, :, :, 1], "y", 0)
    first_half = scatter_axis(scatter_axis(first_half, "y", 0, jnp.bfloat16), "zh", 0)
    second_half = scatter_axis(scatter_axis(second_half, "x", 1, jnp.bfloat16), "zh", 0)
    part = jnp.concatenate([first_half, second_half], axis=0)
    part = part + lax.ppermute(part, REP, chip_pairs(nrep))
    part_other = lax.ppermute(part, REP, core_pairs(nrep))
    first = jnp.where(core == 0, part, part_other)
    second = jnp.where(core == 0, part_other, part)
    reduced = jnp.stack([first, second], axis=1)
    return (outputs, input_grads, reduced)


def shift_pairs(n, k):
    return [(j, (j + k) % n) for j in range(n)]


def gather_axis(a, axis):
    n = lax.axis_size(axis)
    i = lax.axis_index(axis)
    rows = a.shape[0]
    out = jnp.zeros((n * rows,) + a.shape[1:], a.dtype)
    out = lax.dynamic_update_slice_in_dim(out, a, i * rows, 0)
    for k in range(1, n):
        got = lax.ppermute(a, axis, shift_pairs(n, k))
        out = lax.dynamic_update_slice_in_dim(out, got, ((i - k) % n) * rows, 0)
    return out


def scatter_axis(a, axis, dim=0, wire=None):
    n = lax.axis_size(axis)
    i = lax.axis_index(axis)
    total = lax.dynamic_index_in_dim(a, i, dim, keepdims=False).astype(jnp.float32)
    for k in range(1, n):
        chunk = lax.dynamic_index_in_dim(a, (i + k) % n, dim, keepdims=False)
        if wire is not None:
            chunk = chunk.astype(wire)
        total = total + lax.ppermute(chunk, axis, shift_pairs(n, k)).astype(total.dtype)
    return total


def physical_mesh(mesh):
    devices = np.asarray(mesh.devices)
    flat = devices.reshape(-1)
    nx = len({d.coords[0] for d in flat})
    ny = len({d.coords[1] for d in flat})
    nshard, nrep = mesh.shape["shard"], mesh.shape["rep"]
    shape = (ny, nshard // (nx * ny), nx, nrep // 2, 2)
    return Mesh(devices.reshape(shape), SHARD + REP)


def solution(mesh):
    rows = P(SHARD + REP, None)
    in_specs = (rows, rows, rows, P(SHARD, None, None))
    out_specs = (rows, rows, P(SHARD, None, None))
    return jax.shard_map(
        local, mesh=physical_mesh(mesh), in_specs=in_specs, out_specs=out_specs, check_vma=False
    )
```
